512 devices in a mesh: blk: 64 (over z_hi, y, core), seq: 4 (over x), mp: 2 (over z_lo).
Axes of the slice: x: 4, y: 8, z: 8 (z_hi: 4, z_lo: 2; z = z_hi * 2 + z_lo), core: 2. Of those that a mesh axis runs over, the one named last changes fastest.
Arguments:
- hidden: bfloat16 [8, 512, 1536], P(('mp', 'seq'), 'blk'), parts along dimension 0, may hold values from -6 to 6
- labels: int32 [4, 512], P('seq'), may hold values from 0 to 50303
- lengths: int32 [4, 8], P('seq'), may hold values from 1 to 256, 512 in all within a row
- owners: int32 [32], replicated, may hold values from 0 to 31, each once
- w_inner: bfloat16 [3072, 2, 3072], P('mp', None, 'blk'), parts along dimension 0, may hold values from -0.15625 to 0.15625
- w_bcdt: bfloat16 [3072, 304], P('mp'), parts along dimension 0, may hold values from -0.15625 to 0.15625
- conv_inner: float32 [8, 3072], P('mp', 'blk'), parts along dimension 0, may hold values from -3 to 3
- conv_bc: float32 [8, 256], P('mp'), parts along dimension 0, may hold values from -3 to 3
- dt_bias: float32 [96], P('mp'), parts along dimension 0, may hold values from -3 to 0.5
- decay_rate: float32 [96], P('mp'), parts along dimension 0, may hold values from 0.01 to 1
- d_skip: float32 [96], P('mp'), parts along dimension 0, may hold values from 0.5 to 2
- norm_gain: float32 [6144], P(('mp', 'blk')), parts along dimension 0, may hold values from 0.5 to 1.5
- w_out: bfloat16 [6144, 1536], P(('mp', 'blk')), parts along dimension 0, may hold values from -0.109375 to 0.109375
- final_gain: float32 [3072], P('mp'), parts along dimension 0, may hold values from 0.5 to 1.5
- w_head: bfloat16 [3072, 50304], P('mp', 'blk'), parts along dimension 0, may hold values from -0.33170174 to 0.33170174
Outputs:
- layer_out: bfloat16 [8, 512, 1536], P(('mp', 'seq'), 'blk'), parts along dimension 0
- token_logprob: float32 [8, 512], P(('mp', 'seq'), 'blk'), parts along dimension 0
- seq_logprob: float32 [64], P(('mp', 'seq')), parts along dimension 0
The draws below stay inside these ranges and needn't reach their ends.
There are 2 independent parts, one for each index of `mp`. The reference program is written for one: setup_inputs(seed, part) draws one part's arguments, and reference() takes and returns one part's arrays. A program takes and returns all parts, laid end to end along the dimension named above; an argument that names none is the same for every part. Nothing has to cross between parts.
Inputs may be any that keep to these rules, and one draw needn't show every extreme that they name: The 8 lengths of a group sum to 512 and the longest is exactly 256. `owners`: every output slot is named once.
All inputs are finite; a program needn't handle non-finite values.
Results may differ from the reference program's by a relative error of at most 0.0055.
Values may be sent and summed in bfloat16 or wider, within the bound.
No kernel may reach another device: no remote copies, remote signals or barrier semaphores. Data moves between devices by JAX's collectives and lax.ppermute only.
A program may use at most 64 MiB of HBM per device.

```python
import math
import jax
import jax.numpy as jnp
import numpy as np
from jax import lax

D = 1536
HEADDIM = 64
NSTATE = 128
CONV = 4
T_SEQ = 512
SEQS = 8
INNER = 3072
HEADS = 48
VOCAB = 50304
LONG = 256
GROUPS = 4


def draw_hidden(key, part):
    shape = (GROUPS, T_SEQ, D)
    values = jnp.clip(jax.random.normal(jax.random.fold_in(key, 10), shape, jnp.float32), -6.0, 6.0)
    return values.astype(jnp.bfloat16)


def draw_w_head(key, part):
    shape = (D, VOCAB)
    spread_scale = 3.2 / math.sqrt(D)
    values = jnp.clip(jax.random.normal(jax.random.fold_in(key, 20), shape, jnp.float32), -4.0, 4.0) * spread_scale
    return values.astype(jnp.bfloat16)


def with_ends(values, stream_key, smallest, largest):
    longest = values.shape.index(max(values.shape))
    spots = []
    for shift in (0, 1):
        where = [jax.random.randint(jax.random.fold_in(stream_key, axis), (), 0, length) for axis, length in enumerate(values.shape)]
        where[longest] = (where[longest] + shift) % values.shape[longest]
        spots.append(tuple(where))
    return values.at[spots[0]].set(smallest).at[spots[1]].set(largest)


def level_of(key, extent, pieces, low, top_value):
    def one(dim, shards_of):
        heights = jax.random.uniform(jax.random.fold_in(jax.random.fold_in(key, 6), dim), (shards_of,), jnp.float32, low / len(pieces), top_value / len(pieces))
        return jnp.repeat(jnp.exp(heights), extent[dim] // shards_of).reshape((-1,) + (1,) * (len(extent) - dim - 1))

    level = one(*pieces[0])
    for cut in pieces[1:]:
        level = level * one(*cut)
    return level


def rank_table(amount, lean):
    portions = [(1 << 20) // math.isqrt(grade ** lean) + 1 for grade in range(1, amount + 1)]
    scale = 1 + sum(portions) // (1 << 30)
    return np.cumsum(np.array([max(1, weight // scale) for weight in portions]))


def ranked_ids(stream_key, extent, number_of, lean):
    table = rank_table(number_of, lean)
    ticket = jax.random.randint(jax.random.fold_in(stream_key, 1), extent, 0, int(table[number_of - 1]))
    grade = jnp.searchsorted(jnp.asarray(table, jnp.int32), ticket, side="right")
    return jax.random.permutation(jax.random.fold_in(stream_key, 2), number_of)[grade].astype(jnp.int32)


def profile(amount, total, bound, lean):
    weights = [(1 << 20) // math.isqrt(standing ** lean) + 1 for standing in range(2, amount + 1)]
    spare, given = total - bound - (amount - 1), [1] * (amount - 1)
    while spare > 0:
        free = [i for i in range(amount - 1) if given[i] < bound]
        pool, left = sum([weights[i] for i in free]), spare
        for i in free:
            more = min(bound - given[i], max(1, left * weights[i] // pool), spare)
            given[i] = given[i] + more
            spare = spare - more
    return np.array([bound] + given)


def uneven_parts(stream_key, count, total, most, skew):
    if count == 2:
        one = jax.random.randint(stream_key, (), max(1, total - most), min(most, total - 1) + 1)
        return jnp.stack([one, total - one])
    sizes = jnp.asarray(profile(count, total, most, skew), jnp.int32)
    couples = (count - 1) // 2
    source_of, taker = sizes[1:1 + 2 * couples:2], sizes[2:2 + 2 * couples:2]
    room = jnp.minimum(source_of - 1, most - taker)
    shifted = jax.random.randint(jax.random.fold_in(stream_key, 1), (couples,), 0, 1 << 20) % (room + 1)
    sizes = sizes.at[1:1 + 2 * couples:2].set(source_of - shifted).at[2:2 + 2 * couples:2].set(taker + shifted)
    return sizes[jax.random.permutation(jax.random.fold_in(stream_key, 2), count)]


def normal_values(stream_key, dims, deviation, bound, pieces=(), kind=jnp.bfloat16):
    factor_of = level_of(stream_key, dims, pieces, -0.22, 0.18) if pieces else 1.0
    entries = jax.random.normal(stream_key, dims, jnp.float32) * deviation * factor_of
    return jnp.minimum(jnp.maximum(entries, -bound), bound).astype(kind)


def setup_inputs(seed: int = 0, part: int = 0) -> dict:
    key_list = jax.random.split(jax.random.key(seed), 16)
    part_keys = jax.random.split(jax.random.fold_in(key_list[15], part), 16)
    return {
        "hidden": draw_hidden(jax.random.fold_in(jax.random.fold_in(key_list[15], part), 71), part),
        "labels": with_ends(ranked_ids(key_list[1], (GROUPS, T_SEQ), VOCAB, 2), jax.random.fold_in(key_list[1], 3), 0, VOCAB - 1).astype(jnp.int32),
        "lengths": jax.vmap(lambda own: uneven_parts(own, SEQS, T_SEQ, LONG, 2))(jax.random.split(key_list[2], GROUPS)).reshape((GROUPS, SEQS)).astype(jnp.int32),
        "owners": jax.random.permutation(key_list[3], GROUPS * SEQS).astype(jnp.int32),
        "w_inner": normal_values(part_keys[4], (D, 2, INNER), D ** -0.5, 0.15625, ((2, 64),)),
        "w_bcdt": normal_values(part_keys[5], (D, 2 * NSTATE + HEADS), D ** -0.5, 0.15625),
        "conv_inner": normal_values(part_keys[6], (CONV, INNER), CONV ** -0.5, 3.0, ((1, 64),), jnp.float32),
        "conv_bc": normal_values(part_keys[7], (CONV, 2 * NSTATE), CONV ** -0.5, 3.0, (), jnp.float32),
        "dt_bias": jnp.clip(jax.random.uniform(part_keys[8], (HEADS,), jnp.float32, -3.0, 0.5), -3.0, 0.5),
        "decay_rate": jnp.clip(jnp.exp(jax.random.uniform(part_keys[9], (HEADS,), jnp.float32, math.log(0.01), math.log(1.0))), 0.01, 1.0),
        "d_skip": jnp.clip(jax.random.uniform(part_keys[10], (HEADS,), jnp.float32, 0.5, 2.0), 0.5, 2.0),
        "norm_gain": jnp.clip(1.0 + 0.1 * jax.random.normal(part_keys[11], (INNER,), jnp.float32), 0.5, 1.5),
        "w_out": normal_values(part_keys[12], (INNER, D), INNER ** -0.5, 0.109375, ((0, 64),)),
        "final_gain": jnp.clip(1.0 + 0.1 * jax.random.normal(part_keys[13], (D,), jnp.float32), 0.5, 1.5),
        "w_head": draw_w_head(jax.random.fold_in(jax.random.fold_in(key_list[15], part), 71), part),
    }


EPSILON = 1e-05
HIGH = lax.Precision.HIGHEST

def segments_of(lengths):
    starts = jnp.cumsum(lengths, axis=-1) - lengths
    places = jnp.arange(T_SEQ, dtype=jnp.int32)
    segment = lax.optimization_barrier(jnp.sum((places[:, None] >= starts[..., None, :]).astype(jnp.int32), axis=-1)) - 1
    first = jnp.take_along_axis(starts, segment, axis=-1)
    return (segment, places - first)

def causal_conv(values, weights, position):
    total = values * weights[0]
    for shift_by in range(1, CONV):
        moved = jnp.concatenate([jnp.zeros_like(values[..., :shift_by, :]), values[..., :-shift_by, :]], axis=-2)
        total = total + moved * weights[shift_by] * (position >= shift_by).astype(jnp.float32)[..., None]
    return total

def final_norm(values, gain):
    widened = values.astype(jnp.float32)
    scale = lax.rsqrt(lax.optimization_barrier(jnp.mean(widened * widened, axis=-1, keepdims=True)) + EPSILON)
    return (widened * scale * gain).astype(jnp.bfloat16)

def time_major(array):
    return jnp.swapaxes(array, 0, 1)

def reference(hidden, labels, lengths, owners, w_inner, w_bcdt, conv_inner, conv_bc, dt_bias, decay_rate, d_skip, norm_gain, w_out, final_gain, w_head):
    flat = hidden.reshape(GROUPS * T_SEQ, D)
    inner_proj = jnp.dot(flat, w_inner.reshape(D, 2 * INNER), preferred_element_type=jnp.float32).astype(jnp.bfloat16)
    inner_proj = inner_proj.reshape(GROUPS, T_SEQ, 2 * INNER)
    state_proj = jnp.dot(flat, w_bcdt, preferred_element_type=jnp.float32).astype(jnp.bfloat16)
    state_proj = state_proj.reshape(GROUPS, T_SEQ, 2 * NSTATE + HEADS)
    gate_half = inner_proj[..., :INNER].astype(jnp.float32)
    segment, position = segments_of(lengths)
    conv_value = jax.nn.silu(causal_conv(inner_proj[..., INNER:].astype(jnp.float32), conv_inner, position))
    conv_state = jax.nn.silu(causal_conv(state_proj[..., :2 * NSTATE].astype(jnp.float32), conv_bc, position))
    input_map = conv_state[..., :NSTATE]
    output_map = conv_state[..., NSTATE:]
    step_size = jax.nn.softplus(state_proj[..., 2 * NSTATE:].astype(jnp.float32) + dt_bias)
    channel_head = jnp.arange(INNER) // HEADDIM
    log_decay = -(step_size * decay_rate)[..., channel_head]
    driven = conv_value * step_size[..., channel_head]
    keep = (position > 0).astype(jnp.float32)

    def advance(carried, inputs):
        decay_now, drive_now, in_now, out_now, keep_now = inputs
        factor = jnp.exp(decay_now) * keep_now[:, None]
        carried = carried * factor[:, :, None] + drive_now[:, :, None] * in_now[:, None, :]
        return (carried, lax.optimization_barrier(jnp.sum(carried * out_now[:, None, :], axis=-1)))
    initial = jnp.zeros((GROUPS, INNER, NSTATE), jnp.float32)
    final_state, scanned = lax.scan(advance, initial, (time_major(log_decay), time_major(driven), time_major(input_map), time_major(output_map), time_major(keep)))
    mixed = time_major(scanned) + d_skip[channel_head] * conv_value
    gated = mixed * jax.nn.silu(gate_half)
    scale = lax.rsqrt(lax.optimization_barrier(jnp.mean(gated * gated, axis=-1, keepdims=True)) + EPSILON)
    gated_norm = (gated * scale * norm_gain).astype(jnp.bfloat16).reshape(GROUPS * T_SEQ, INNER)
    delta = jnp.dot(gated_norm, w_out, preferred_element_type=jnp.float32)
    layer_out = (flat.astype(jnp.float32) + delta).astype(jnp.bfloat16)
    normed = final_norm(layer_out, final_gain).reshape(GROUPS, T_SEQ, D)

    def score(rows):
        normed_rows, label_rows = rows
        logits = jnp.dot(normed_rows, w_head, preferred_element_type=jnp.float32)
        total = jax.nn.logsumexp(logits, axis=-1)
        target = jnp.take_along_axis(logits, label_rows[:, None], axis=-1)[:, 0]
        return target - total
    token_logprob = lax.map(score, (normed, labels))
    onehot = (segment[..., None] == jnp.arange(SEQS, dtype=jnp.int32)).astype(jnp.float32)
    sums = jnp.einsum('gt,gts->gs', token_logprob, onehot, precision=HIGH)
    seq_logprob = jnp.zeros((GROUPS * SEQS,), jnp.float32).at[owners].set(sums.reshape(-1))
    return (layer_out.reshape(GROUPS, T_SEQ, D), token_logprob, seq_logprob)
```

```python
import jax
import jax.numpy as jnp
from jax import lax
from jax.sharding import Mesh
from jax.sharding import PartitionSpec as P

D = 1536
HEADDIM = 64
NSTATE = 128
SCAN_BLOCK = 256
CONV = 4


EPSILON = 1e-05
HIGH = lax.Precision.HIGHEST
BLK = ("bz", "by", "bc")


def gather_rows(rows):
    part = lax.all_gather(rows, "bz", axis=0)
    part = lax.all_gather(part, "by", axis=1)
    part = lax.all_gather(part, "bc", axis=2)
    return part.reshape((-1,) + rows.shape[1:])


def scatter_rows(values):
    bz = lax.axis_size("bz")
    by = lax.axis_size("by")
    bc = lax.axis_size("bc")
    part = values.reshape((bz, by, bc, -1) + values.shape[1:])
    part = lax.psum_scatter(part, "bc", scatter_dimension=2)
    part = lax.psum_scatter(part, "by", scatter_dimension=1)
    return lax.psum_scatter(part, "bz", scatter_dimension=0)


def sum_blk(values):
    return lax.psum(lax.psum(lax.psum(values, "bc"), "by"), "bz")


def max_blk(values):
    return lax.pmax(lax.pmax(lax.pmax(values, "bc"), "by"), "bz")


def segments_of(lengths, count):
    starts = jnp.cumsum(lengths, axis=-1) - lengths
    places = jnp.arange(count, dtype=jnp.int32)
    segment = jnp.sum((places[:, None] >= starts[None, :]).astype(jnp.int32), axis=-1) - 1
    first = jnp.take(starts, segment)
    return (segment, places - first)


def causal_conv(values, weights, position):
    total = values * weights[0]
    for shift_by in range(1, CONV):
        moved = jnp.concatenate(
            [jnp.zeros_like(values[:shift_by, :]), values[:-shift_by, :]], axis=0
        )
        total = (
            total + moved * weights[shift_by] * (position >= shift_by).astype(jnp.float32)[:, None]
        )
    return total


def final_norm(values, gain):
    widened = values.astype(jnp.float32)
    scale = lax.rsqrt(jnp.mean(widened * widened, axis=-1, keepdims=True) + EPSILON)
    return (widened * scale * gain).astype(jnp.bfloat16)


def shards(
    hidden,
    labels,
    lengths,
    owners,
    w_inner,
    w_bcdt,
    conv_inner,
    conv_bc,
    dt_bias,
    decay_rate,
    d_skip,
    norm_gain,
    w_out,
    final_gain,
    w_head,
):
    rows_own = hidden[0]
    rows_count = rows_own.shape[0]
    blk_count = lax.axis_size("bz") * lax.axis_size("by") * lax.axis_size("bc")
    blk_index = (
        lax.axis_index("bz") * lax.axis_size("by") + lax.axis_index("by")
    ) * lax.axis_size("bc") + lax.axis_index("bc")
    gathered = gather_rows(rows_own)
    tokens_all = gathered.shape[0]
    channels = w_inner.shape[2]
    inner_total = channels * blk_count
    inner_proj = jnp.dot(
        gathered, w_inner.reshape(D, 2 * channels), preferred_element_type=jnp.float32
    ).astype(jnp.bfloat16)
    state_proj = jnp.dot(gathered, w_bcdt, preferred_element_type=jnp.float32).astype(jnp.bfloat16)
    gate_half = inner_proj[:, :channels].astype(jnp.float32)
    segment, position = segments_of(lengths[0], tokens_all)
    conv_value = jax.nn.silu(
        causal_conv(inner_proj[:, channels:].astype(jnp.float32), conv_inner, position)
    )
    conv_state = jax.nn.silu(
        causal_conv(state_proj[:, : 2 * NSTATE].astype(jnp.float32), conv_bc, position)
    )
    input_map = conv_state[:, :NSTATE]
    output_map = conv_state[:, NSTATE:]
    step_size = jax.nn.softplus(state_proj[:, 2 * NSTATE :].astype(jnp.float32) + dt_bias)
    log_heads = -(step_size * decay_rate)
    first_channel = blk_index * channels
    channel_head = (first_channel + jnp.arange(channels, dtype=jnp.int32)) // HEADDIM
    head_low = first_channel // HEADDIM
    head_high = (first_channel + channels - 1) // HEADDIM
    mask_high = (channel_head == head_high).astype(jnp.float32)
    mask_low = 1.0 - mask_high
    step_pair = jnp.concatenate(
        [
            lax.dynamic_slice_in_dim(step_size, head_low, 1, 1),
            lax.dynamic_slice_in_dim(step_size, head_high, 1, 1),
        ],
        axis=1,
    )
    log_pair = jnp.concatenate(
        [
            lax.dynamic_slice_in_dim(log_heads, head_low, 1, 1),
            lax.dynamic_slice_in_dim(log_heads, head_high, 1, 1),
        ],
        axis=1,
    )
    step_channel = step_pair[:, 0:1] * mask_low + step_pair[:, 1:2] * mask_high
    driven = conv_value * step_channel
    slot_masks = (mask_low, mask_high)
    blocks = tokens_all // SCAN_BLOCK
    order = jnp.arange(SCAN_BLOCK, dtype=jnp.int32)
    causal = order[:, None] >= order[None, :]

    def block_step(carry, inputs):
        carried, previous = carry
        drive_block, in_block, out_block, log_block, seg_block = inputs
        cumulative = jnp.cumsum(log_block, axis=0)
        gram = jnp.dot(out_block, in_block.T, precision=HIGH)
        same = (seg_block[:, None] == seg_block[None, :]) & causal
        result = jnp.zeros((SCAN_BLOCK, channels), jnp.float32)
        for slot_index in range(2):
            column = cumulative[:, slot_index]
            spread = jnp.minimum(column[:, None] - column[None, :], 0.0)
            weights = jnp.where(same, jnp.exp(spread), 0.0)
            result = result + jnp.dot(
                gram * weights, drive_block * slot_masks[slot_index], precision=HIGH
            )
        carried_in = carried * (seg_block[0] == previous).astype(jnp.float32)
        rising = jnp.exp(cumulative[:, 0:1]) * mask_low + jnp.exp(cumulative[:, 1:2]) * mask_high
        leading = (seg_block == seg_block[0]).astype(jnp.float32)[:, None]
        result = result + leading * rising * jnp.dot(out_block, carried_in.T, precision=HIGH)
        trailing = (seg_block == seg_block[-1]).astype(jnp.float32)[:, None]
        tail_low = jnp.exp(cumulative[-1:, 0:1] - cumulative[:, 0:1])
        tail_high = jnp.exp(cumulative[-1:, 1:2] - cumulative[:, 1:2])
        tail = tail_low * mask_low + tail_high * mask_high
        whole_block = (seg_block[-1] == seg_block[0]).astype(jnp.float32)
        carried_new = whole_block * rising[-1][:, None] * carried_in + jnp.dot(
            (drive_block * tail * trailing).T, in_block, precision=HIGH
        )
        return ((carried_new, seg_block[-1]), result)

    initial = (jnp.zeros((channels, NSTATE), jnp.float32), jnp.int32(-1))
    scan_inputs = (
        driven.reshape(blocks, SCAN_BLOCK, channels),
        input_map.reshape(blocks, SCAN_BLOCK, NSTATE),
        output_map.reshape(blocks, SCAN_BLOCK, NSTATE),
        log_pair.reshape(blocks, SCAN_BLOCK, 2),
        segment.reshape(blocks, SCAN_BLOCK),
    )
    final_carry, scanned = lax.scan(block_step, initial, scan_inputs)
    mixed = scanned.reshape(tokens_all, channels) + jnp.take(d_skip, channel_head) * conv_value
    gated = mixed * jax.nn.silu(gate_half)
    squares = sum_blk(jnp.sum(gated * gated, axis=1))
    inverse = lax.rsqrt(squares / inner_total + EPSILON)
    gated_norm = (gated * inverse[:, None] * norm_gain).astype(jnp.bfloat16)
    delta_own = scatter_rows(jnp.dot(gated_norm, w_out, preferred_element_type=jnp.float32))
    layer_own = (rows_own.astype(jnp.float32) + delta_own).astype(jnp.bfloat16)
    logits = jnp.dot(
        gather_rows(final_norm(layer_own, final_gain)),
        w_head,
        preferred_element_type=jnp.float32,
    )
    vocab_local = w_head.shape[1]
    local_label = labels[0] - blk_index * vocab_local
    hit = jnp.arange(vocab_local, dtype=jnp.int32)[None, :] == local_label[:, None]
    target_local = jnp.sum(jnp.where(hit, logits, 0.0), axis=1)
    top_local = jnp.max(logits, axis=1)
    top_all = max_blk(top_local)
    expsum_local = jnp.sum(jnp.exp(logits - top_all[:, None]), axis=1)
    expsum_all, target_all = sum_blk((expsum_local, target_local))
    logprob = target_all - (top_all + jnp.log(expsum_all))
    token_own = lax.dynamic_slice_in_dim(logprob, blk_index * rows_count, rows_count, 0)
    seqs_count = lengths.shape[1]
    onehot = (segment[:, None] == jnp.arange(seqs_count, dtype=jnp.int32)[None, :]).astype(
        jnp.float32
    )
    sums = jnp.dot(logprob, onehot, precision=HIGH)
    seq_index = lax.axis_index("seq")
    mine = lax.dynamic_slice_in_dim(owners, seq_index * seqs_count, seqs_count, 0)
    placement = (mine[:, None] == jnp.arange(owners.shape[0], dtype=jnp.int32)[None, :]).astype(
        jnp.float32
    )
    spread_sums = jnp.dot(sums, placement, precision=HIGH)
    seq_own = lax.psum_scatter(spread_sums, "seq", scatter_dimension=0, tiled=True)
    return (layer_own[None], token_own[None], seq_own)


def solution(mesh):
    blk = mesh.shape["blk"]
    split = mesh.devices.reshape((blk // 16, 8, 2) + mesh.devices.shape[1:])
    mesh = Mesh(split, BLK + mesh.axis_names[1:])
    in_specs = (
        P(("mp", "seq"), BLK, None),
        P("seq", None),
        P("seq", None),
        P(),
        P("mp", None, BLK),
        P("mp", None),
        P("mp", BLK),
        P("mp", None),
        P("mp"),
        P("mp"),
        P("mp"),
        P(("mp",) + BLK),
        P(("mp",) + BLK, None),
        P("mp"),
        P("mp", BLK),
    )
    out_specs = (P(("mp", "seq"), BLK, None), P(("mp", "seq"), BLK), P(("mp", "seq")))
    return jax.shard_map(shards, mesh=mesh, in_specs=in_specs, out_specs=out_specs, check_vma=False)
```

```python
import jax
import jax.numpy as jnp
from jax import lax
from jax.sharding import Mesh
from jax.sharding import PartitionSpec as P

D = 1536
HEADDIM = 64
NSTATE = 128
SCAN_BLOCK = 256
CONV = 4


EPSILON = 1e-05
HIGH = lax.Precision.HIGHEST
BLK = ("bz", "by", "bc")


def gather_rows(rows):
    part = lax.all_gather(rows, "bz", axis=0)
    part = lax.all_gather(part, "by", axis=1)
    part = lax.all_gather(part, "bc", axis=2)
    return part.reshape((-1,) + rows.shape[1:])


def scatter_rows(values):
    bz = lax.axis_size("bz")
    by = lax.axis_size("by")
    bc = lax.axis_size("bc")
    part = values.reshape((bz, by, bc, -1) + values.shape[1:])
    part = lax.psum_scatter(part, "bc", scatter_dimension=2)
    part = lax.psum_scatter(part, "by", scatter_dimension=1)
    return lax.psum_scatter(part, "bz", scatter_dimension=0)


def sum_blk(values):
    return lax.psum(lax.psum(lax.psum(values, "bc"), "by"), "bz")


def combine_blk(top, expsum, target):
    for axis in ("bc", "by", "bz"):
        pieces = lax.all_gather(jnp.stack([top, expsum, target]), axis, axis=0)
        top = jnp.max(pieces[:, 0], axis=0)
        expsum = jnp.sum(pieces[:, 1] * jnp.exp(pieces[:, 0] - top[None]), axis=0)
        target = jnp.sum(pieces[:, 2], axis=0)
    return top, expsum, target


def segments_of(lengths, count):
    starts = jnp.cumsum(lengths, axis=-1) - lengths
    places = jnp.arange(count, dtype=jnp.int32)
    segment = jnp.sum((places[:, None] >= starts[None, :]).astype(jnp.int32), axis=-1) - 1
    first = jnp.take(starts, segment)
    return (segment, places - first)


def causal_conv(values, weights, position):
    total = values * weights[0]
    for shift_by in range(1, CONV):
        moved = jnp.concatenate(
            [jnp.zeros_like(values[:shift_by, :]), values[:-shift_by, :]], axis=0
        )
        total = (
            total + moved * weights[shift_by] * (position >= shift_by).astype(jnp.float32)[:, None]
        )
    return total


def final_norm(values, gain):
    widened = values.astype(jnp.float32)
    scale = lax.rsqrt(jnp.mean(widened * widened, axis=-1, keepdims=True) + EPSILON)
    return (widened * scale * gain).astype(jnp.bfloat16)


def shards(
    hidden,
    labels,
    lengths,
    owners,
    w_inner,
    w_bcdt,
    conv_inner,
    conv_bc,
    dt_bias,
    decay_rate,
    d_skip,
    norm_gain,
    w_out,
    final_gain,
    w_head,
):
    rows_own = hidden[0]
    rows_count = rows_own.shape[0]
    blk_count = lax.axis_size("bz") * lax.axis_size("by") * lax.axis_size("bc")
    blk_index = (
        lax.axis_index("bz") * lax.axis_size("by") + lax.axis_index("by")
    ) * lax.axis_size("bc") + lax.axis_index("bc")
    gathered = gather_rows(rows_own)
    tokens_all = gathered.shape[0]
    channels = w_inner.shape[2]
    inner_total = channels * blk_count
    inner_proj = jnp.dot(
        gathered, w_inner.reshape(D, 2 * channels), preferred_element_type=jnp.float32
    ).astype(jnp.bfloat16)
    state_proj = jnp.dot(gathered, w_bcdt, preferred_element_type=jnp.float32).astype(jnp.bfloat16)
    gate_half = inner_proj[:, :channels].astype(jnp.float32)
    segment, position = segments_of(lengths[0], tokens_all)
    conv_value = jax.nn.silu(
        causal_conv(inner_proj[:, channels:].astype(jnp.float32), conv_inner, position)
    )
    conv_state = jax.nn.silu(
        causal_conv(state_proj[:, : 2 * NSTATE].astype(jnp.float32), conv_bc, position)
    )
    input_map = conv_state[:, :NSTATE]
    output_map = conv_state[:, NSTATE:]
    step_size = jax.nn.softplus(state_proj[:, 2 * NSTATE :].astype(jnp.float32) + dt_bias)
    log_heads = -(step_size * decay_rate)
    first_channel = blk_index * channels
    channel_head = (first_channel + jnp.arange(channels, dtype=jnp.int32)) // HEADDIM
    head_low = first_channel // HEADDIM
    head_high = (first_channel + channels - 1) // HEADDIM
    mask_high = (channel_head == head_high).astype(jnp.float32)
    mask_low = 1.0 - mask_high
    step_pair = jnp.concatenate(
        [
            lax.dynamic_slice_in_dim(step_size, head_low, 1, 1),
            lax.dynamic_slice_in_dim(step_size, head_high, 1, 1),
        ],
        axis=1,
    )
    log_pair = jnp.concatenate(
        [
            lax.dynamic_slice_in_dim(log_heads, head_low, 1, 1),
            lax.dynamic_slice_in_dim(log_heads, head_high, 1, 1),
        ],
        axis=1,
    )
    step_channel = step_pair[:, 0:1] * mask_low + step_pair[:, 1:2] * mask_high
    driven = conv_value * step_channel
    slot_masks = (mask_low, mask_high)
    blocks = tokens_all // SCAN_BLOCK
    order = jnp.arange(SCAN_BLOCK, dtype=jnp.int32)
    causal = order[:, None] >= order[None, :]

    def block_step(carry, inputs):
        carried, previous = carry
        drive_block, in_block, out_block, log_block, seg_block = inputs
        cumulative = jnp.cumsum(log_block, axis=0)
        gram = jnp.dot(out_block, in_block.T, precision=HIGH)
        same = (seg_block[:, None] == seg_block[None, :]) & causal
        result = jnp.zeros((SCAN_BLOCK, channels), jnp.float32)
        for slot_index in range(2):
            column = cumulative[:, slot_index]
            spread = jnp.minimum(column[:, None] - column[None, :], 0.0)
            weights = jnp.where(same, jnp.exp(spread), 0.0)
            result = result + jnp.dot(
                gram * weights, drive_block * slot_masks[slot_index], precision=HIGH
            )
        carried_in = carried * (seg_block[0] == previous).astype(jnp.float32)
        rising = jnp.exp(cumulative[:, 0:1]) * mask_low + jnp.exp(cumulative[:, 1:2]) * mask_high
        leading = (seg_block == seg_block[0]).astype(jnp.float32)[:, None]
        result = result + leading * rising * jnp.dot(out_block, carried_in.T, precision=HIGH)
        trailing = (seg_block == seg_block[-1]).astype(jnp.float32)[:, None]
        tail_low = jnp.exp(cumulative[-1:, 0:1] - cumulative[:, 0:1])
        tail_high = jnp.exp(cumulative[-1:, 1:2] - cumulative[:, 1:2])
        tail = tail_low * mask_low + tail_high * mask_high
        whole_block = (seg_block[-1] == seg_block[0]).astype(jnp.float32)
        carried_new = whole_block * rising[-1][:, None] * carried_in + jnp.dot(
            (drive_block * tail * trailing).T, in_block, precision=HIGH
        )
        return ((carried_new, seg_block[-1]), result)

    initial = (jnp.zeros((channels, NSTATE), jnp.float32), jnp.int32(-1))
    scan_inputs = (
        driven.reshape(blocks, SCAN_BLOCK, channels),
        input_map.reshape(blocks, SCAN_BLOCK, NSTATE),
        output_map.reshape(blocks, SCAN_BLOCK, NSTATE),
        log_pair.reshape(blocks, SCAN_BLOCK, 2),
        segment.reshape(blocks, SCAN_BLOCK),
    )
    final_carry, scanned = lax.scan(block_step, initial, scan_inputs)
    mixed = scanned.reshape(tokens_all, channels) + jnp.take(d_skip, channel_head) * conv_value
    gated = mixed * jax.nn.silu(gate_half)
    squares = jnp.sum(gated * gated, axis=1)
    gained = (gated * norm_gain).astype(jnp.bfloat16)
    partial = jnp.dot(gained, w_out, preferred_element_type=jnp.float32)
    packed = jnp.concatenate(
        [partial, squares[:, None], jnp.zeros((tokens_all, 127), jnp.float32)], axis=1
    )
    packed_own = scatter_rows(packed)
    inverse = lax.rsqrt(packed_own[:, D] / inner_total + EPSILON)
    delta_own = packed_own[:, :D] * inverse[:, None]
    layer_own = (rows_own.astype(jnp.float32) + delta_own).astype(jnp.bfloat16)
    logits = jnp.dot(
        gather_rows(final_norm(layer_own, final_gain)),
        w_head,
        preferred_element_type=jnp.float32,
    )
    vocab_local = w_head.shape[1]
    local_label = labels[0] - blk_index * vocab_local
    hit = jnp.arange(vocab_local, dtype=jnp.int32)[None, :] == local_label[:, None]
    target_local = jnp.sum(jnp.where(hit, logits, 0.0), axis=1)
    top_local = jnp.max(logits, axis=1)
    expsum_local = jnp.sum(jnp.exp(logits - top_local[:, None]), axis=1)
    top_all, expsum_all, target_all = combine_blk(top_local, expsum_local, target_local)
    logprob = target_all - (top_all + jnp.log(expsum_all))
    token_own = lax.dynamic_slice_in_dim(logprob, blk_index * rows_count, rows_count, 0)
    seqs_count = lengths.shape[1]
    onehot = (segment[:, None] == jnp.arange(seqs_count, dtype=jnp.int32)[None, :]).astype(
        jnp.float32
    )
    sums = jnp.dot(logprob, onehot, precision=HIGH)
    seq_index = lax.axis_index("seq")
    mine = lax.dynamic_slice_in_dim(owners, seq_index * seqs_count, seqs_count, 0)
    placement = (mine[:, None] == jnp.arange(owners.shape[0], dtype=jnp.int32)[None, :]).astype(
        jnp.float32
    )
    spread_sums = jnp.dot(sums, placement, precision=HIGH)
    seq_own = lax.psum_scatter(spread_sums, "seq", scatter_dimension=0, tiled=True)
    return (layer_own[None], token_own[None], seq_own)


def solution(mesh):
    blk = mesh.shape["blk"]
    split = mesh.devices.reshape((blk // 16, 8, 2) + mesh.devices.shape[1:])
    mesh = Mesh(split, BLK + mesh.axis_names[1:])
    in_specs = (
        P(("mp", "seq"), BLK, None),
        P("seq", None),
        P("seq", None),
        P(),
        P("mp", None, BLK),
        P("mp", None),
        P("mp", BLK),
        P("mp", None),
        P("mp"),
        P("mp"),
        P("mp"),
        P(("mp",) + BLK),
        P(("mp",) + BLK, None),
        P("mp"),
        P("mp", BLK),
    )
    out_specs = (P(("mp", "seq"), BLK, None), P(("mp", "seq"), BLK), P(("mp", "seq")))
    return jax.shard_map(shards, mesh=mesh, in_specs=in_specs, out_specs=out_specs, check_vma=False)
```

```python
import jax
import jax.numpy as jnp
from jax import lax
from jax.sharding import Mesh
from jax.sharding import PartitionSpec as P

D = 1536
HEADDIM = 64
NSTATE = 128
SCAN_BLOCK = 512
CONV = 4


EPSILON = 1e-05
HIGH = lax.Precision.HIGHEST
BLK = ("bz", "by", "bc")


def gather_rows(rows):
    part = lax.all_gather(rows, "bz", axis=0)
    part = lax.all_gather(part, "by", axis=1)
    part = lax.all_gather(part, "bc", axis=2)
    return part.reshape((-1,) + rows.shape[1:])


def scatter_rows(values):
    bz = lax.axis_size("bz")
    by = lax.axis_size("by")
    bc = lax.axis_size("bc")
    part = values.reshape((bz, by, bc, -1) + values.shape[1:])
    part = lax.psum_scatter(part, "bc", scatter_dimension=2)
    part = lax.psum_scatter(part, "by", scatter_dimension=1)
    return lax.psum_scatter(part, "bz", scatter_dimension=0)


def sum_blk(values):
    return lax.psum(lax.psum(lax.psum(values, "bc"), "by"), "bz")


def combine_blk(top, expsum, target):
    for axis in ("bc", "by", "bz"):
        pieces = lax.all_gather(jnp.stack([top, expsum, target]), axis, axis=0)
        top = jnp.max(pieces[:, 0], axis=0)
        expsum = jnp.sum(pieces[:, 1] * jnp.exp(pieces[:, 0] - top[None]), axis=0)
        target = jnp.sum(pieces[:, 2], axis=0)
    return top, expsum, target


def segments_of(lengths, count):
    starts = jnp.cumsum(lengths, axis=-1) - lengths
    places = jnp.arange(count, dtype=jnp.int32)
    segment = jnp.sum((places[:, None] >= starts[None, :]).astype(jnp.int32), axis=-1) - 1
    first = jnp.take(starts, segment)
    return (segment, places - first)


def causal_conv(values, weights, position):
    total = values * weights[0]
    for shift_by in range(1, CONV):
        moved = jnp.concatenate(
            [jnp.zeros_like(values[:shift_by, :]), values[:-shift_by, :]], axis=0
        )
        total = (
            total + moved * weights[shift_by] * (position >= shift_by).astype(jnp.float32)[:, None]
        )
    return total


def final_norm(values, gain):
    widened = values.astype(jnp.float32)
    scale = lax.rsqrt(jnp.mean(widened * widened, axis=-1, keepdims=True) + EPSILON)
    return (widened * scale * gain).astype(jnp.bfloat16)


def shards(
    hidden,
    labels,
    lengths,
    owners,
    w_inner,
    w_bcdt,
    conv_inner,
    conv_bc,
    dt_bias,
    decay_rate,
    d_skip,
    norm_gain,
    w_out,
    final_gain,
    w_head,
):
    rows_own = hidden[0]
    rows_count = rows_own.shape[0]
    blk_count = lax.axis_size("bz") * lax.axis_size("by") * lax.axis_size("bc")
    blk_index = (
        lax.axis_index("bz") * lax.axis_size("by") + lax.axis_index("by")
    ) * lax.axis_size("bc") + lax.axis_index("bc")
    gathered = gather_rows(rows_own)
    tokens_all = gathered.shape[0]
    channels = w_inner.shape[2]
    inner_total = channels * blk_count
    inner_proj = jnp.dot(
        gathered, w_inner.reshape(D, 2 * channels), preferred_element_type=jnp.float32
    ).astype(jnp.bfloat16)
    state_proj = jnp.dot(gathered, w_bcdt, preferred_element_type=jnp.float32).astype(jnp.bfloat16)
    gate_half = inner_proj[:, :channels].astype(jnp.float32)
    segment, position = segments_of(lengths[0], tokens_all)
    conv_value = jax.nn.silu(
        causal_conv(inner_proj[:, channels:].astype(jnp.float32), conv_inner, position)
    )
    conv_state = jax.nn.silu(
        causal_conv(state_proj[:, : 2 * NSTATE].astype(jnp.float32), conv_bc, position)
    )
    input_map = conv_state[:, :NSTATE]
    output_map = conv_state[:, NSTATE:]
    step_size = jax.nn.softplus(state_proj[:, 2 * NSTATE :].astype(jnp.float32) + dt_bias)
    log_heads = -(step_size * decay_rate)
    first_channel = blk_index * channels
    channel_head = (first_channel + jnp.arange(channels, dtype=jnp.int32)) // HEADDIM
    head_low = first_channel // HEADDIM
    head_high = (first_channel + channels - 1) // HEADDIM
    mask_high = (channel_head == head_high).astype(jnp.float32)
    mask_low = 1.0 - mask_high
    step_pair = jnp.concatenate(
        [
            lax.dynamic_slice_in_dim(step_size, head_low, 1, 1),
            lax.dynamic_slice_in_dim(step_size, head_high, 1, 1),
        ],
        axis=1,
    )
    log_pair = jnp.concatenate(
        [
            lax.dynamic_slice_in_dim(log_heads, head_low, 1, 1),
            lax.dynamic_slice_in_dim(log_heads, head_high, 1, 1),
        ],
        axis=1,
    )
    step_channel = step_pair[:, 0:1] * mask_low + step_pair[:, 1:2] * mask_high
    driven = conv_value * step_channel
    slot_masks = (mask_low, mask_high)
    blocks = tokens_all // SCAN_BLOCK
    order = jnp.arange(SCAN_BLOCK, dtype=jnp.int32)
    causal = order[:, None] >= order[None, :]

    def block_step(carry, inputs):
        carried, previous = carry
        drive_block, in_block, out_block, log_block, seg_block = inputs
        cumulative = jnp.cumsum(log_block, axis=0)
        gram = jnp.dot(out_block, in_block.T, precision=HIGH)
        same = (seg_block[:, None] == seg_block[None, :]) & causal
        result = jnp.zeros((SCAN_BLOCK, channels), jnp.float32)
        for slot_index in range(2):
            column = cumulative[:, slot_index]
            spread = jnp.minimum(column[:, None] - column[None, :], 0.0)
            weights = jnp.where(same, jnp.exp(spread), 0.0)
            result = result + jnp.dot(
                gram * weights, drive_block * slot_masks[slot_index], precision=HIGH
            )
        carried_in = carried * (seg_block[0] == previous).astype(jnp.float32)
        rising = jnp.exp(cumulative[:, 0:1]) * mask_low + jnp.exp(cumulative[:, 1:2]) * mask_high
        leading = (seg_block == seg_block[0]).astype(jnp.float32)[:, None]
        result = result + leading * rising * jnp.dot(out_block, carried_in.T, precision=HIGH)
        trailing = (seg_block == seg_block[-1]).astype(jnp.float32)[:, None]
        tail_low = jnp.exp(cumulative[-1:, 0:1] - cumulative[:, 0:1])
        tail_high = jnp.exp(cumulative[-1:, 1:2] - cumulative[:, 1:2])
        tail = tail_low * mask_low + tail_high * mask_high
        whole_block = (seg_block[-1] == seg_block[0]).astype(jnp.float32)
        carried_new = whole_block * rising[-1][:, None] * carried_in + jnp.dot(
            (drive_block * tail * trailing).T, in_block, precision=HIGH
        )
        return ((carried_new, seg_block[-1]), result)

    initial = (jnp.zeros((channels, NSTATE), jnp.float32), jnp.int32(-1))
    scan_inputs = (
        driven.reshape(blocks, SCAN_BLOCK, channels),
        input_map.reshape(blocks, SCAN_BLOCK, NSTATE),
        output_map.reshape(blocks, SCAN_BLOCK, NSTATE),
        log_pair.reshape(blocks, SCAN_BLOCK, 2),
        segment.reshape(blocks, SCAN_BLOCK),
    )
    final_carry, scanned = lax.scan(block_step, initial, scan_inputs)
    mixed = scanned.reshape(tokens_all, channels) + jnp.take(d_skip, channel_head) * conv_value
    gated = mixed * jax.nn.silu(gate_half)
    squares = jnp.sum(gated * gated, axis=1)
    gained = (gated * norm_gain).astype(jnp.bfloat16)
    partial = jnp.dot(gained, w_out, preferred_element_type=jnp.float32)
    packed = jnp.concatenate(
        [partial, squares[:, None], jnp.zeros((tokens_all, 127), jnp.float32)], axis=1
    )
    packed_own = scatter_rows(packed)
    inverse = lax.rsqrt(packed_own[:, D] / inner_total + EPSILON)
    delta_own = packed_own[:, :D] * inverse[:, None]
    layer_own = (rows_own.astype(jnp.float32) + delta_own).astype(jnp.bfloat16)
    logits = jnp.dot(
        gather_rows(final_norm(layer_own, final_gain)),
        w_head,
        preferred_element_type=jnp.float32,
    )
    vocab_local = w_head.shape[1]
    local_label = labels[0] - blk_index * vocab_local
    hit = jnp.arange(vocab_local, dtype=jnp.int32)[None, :] == local_label[:, None]
    target_local = jnp.sum(jnp.where(hit, logits, 0.0), axis=1)
    top_local = jnp.max(logits, axis=1)
    expsum_local = jnp.sum(jnp.exp(logits - top_local[:, None]), axis=1)
    top_all, expsum_all, target_all = combine_blk(top_local, expsum_local, target_local)
    logprob = target_all - (top_all + jnp.log(expsum_all))
    token_own = lax.dynamic_slice_in_dim(logprob, blk_index * rows_count, rows_count, 0)
    seqs_count = lengths.shape[1]
    onehot = (segment[:, None] == jnp.arange(seqs_count, dtype=jnp.int32)[None, :]).astype(
        jnp.float32
    )
    sums = jnp.dot(logprob, onehot, precision=HIGH)
    seq_index = lax.axis_index("seq")
    mine = lax.dynamic_slice_in_dim(owners, seq_index * seqs_count, seqs_count, 0)
    placement = (mine[:, None] == jnp.arange(owners.shape[0], dtype=jnp.int32)[None, :]).astype(
        jnp.float32
    )
    spread_sums = jnp.dot(sums, placement, precision=HIGH)
    seq_own = lax.psum_scatter(spread_sums, "seq", scatter_dimension=0, tiled=True)
    return (layer_own[None], token_own[None], seq_own)


def solution(mesh):
    blk = mesh.shape["blk"]
    split = mesh.devices.reshape((blk // 16, 8, 2) + mesh.devices.shape[1:])
    mesh = Mesh(split, BLK + mesh.axis_names[1:])
    in_specs = (
        P(("mp", "seq"), BLK, None),
        P("seq", None),
        P("seq", None),
        P(),
        P("mp", None, BLK),
        P("mp", None),
        P("mp", BLK),
        P("mp", None),
        P("mp"),
        P("mp"),
        P("mp"),
        P(("mp",) + BLK),
        P(("mp",) + BLK, None),
        P("mp"),
        P("mp", BLK),
    )
    out_specs = (P(("mp", "seq"), BLK, None), P(("mp", "seq"), BLK), P(("mp", "seq")))
    return jax.shard_map(shards, mesh=mesh, in_specs=in_specs, out_specs=out_specs, check_vma=False)
```

```python
import jax
import jax.numpy as jnp
from jax import lax
from jax.sharding import Mesh
from jax.sharding import PartitionSpec as P

D = 1536
HEADDIM = 64
NSTATE = 128
SCAN_BLOCK = 512
CONV = 4


EPSILON = 1e-05
HIGH = lax.Precision.HIGHEST
BLK = ("bz", "by", "bc")


def gather_rows(rows):
    part = lax.all_gather(rows, "bz", axis=0)
    part = lax.all_gather(part, "by", axis=1)
    part = lax.all_gather(part, "bc", axis=2)
    return part.reshape((-1,) + rows.shape[1:])


def scatter_rows(values):
    bz = lax.axis_size("bz")
    by = lax.axis_size("by")
    bc = lax.axis_size("bc")
    part = values.reshape((bz, by, bc, -1) + values.shape[1:])
    part = lax.psum_scatter(part, "bc", scatter_dimension=2)
    part = lax.psum_scatter(part, "by", scatter_dimension=1)
    return lax.psum_scatter(part, "bz", scatter_dimension=0)


def sum_blk(values):
    return lax.psum(lax.psum(lax.psum(values, "bc"), "by"), "bz")


def combine_blk(top, expsum, target):
    for axis in ("bc", "by", "bz"):
        pieces = lax.all_gather(jnp.stack([top, expsum, target]), axis, axis=0)
        top = jnp.max(pieces[:, 0], axis=0)
        expsum = jnp.sum(pieces[:, 1] * jnp.exp(pieces[:, 0] - top[None]), axis=0)
        target = jnp.sum(pieces[:, 2], axis=0)
    return top, expsum, target


def segments_of(lengths, count):
    starts = jnp.cumsum(lengths, axis=-1) - lengths
    places = jnp.arange(count, dtype=jnp.int32)
    segment = jnp.sum((places[:, None] >= starts[None, :]).astype(jnp.int32), axis=-1) - 1
    first = jnp.take(starts, segment)
    return (segment, places - first)


def causal_conv(values, weights, position):
    total = values * weights[0]
    for shift_by in range(1, CONV):
        moved = jnp.concatenate(
            [jnp.zeros_like(values[:shift_by, :]), values[:-shift_by, :]], axis=0
        )
        total = (
            total + moved * weights[shift_by] * (position >= shift_by).astype(jnp.float32)[:, None]
        )
    return total


def final_norm(values, gain):
    widened = values.astype(jnp.float32)
    scale = lax.rsqrt(jnp.mean(widened * widened, axis=-1, keepdims=True) + EPSILON)
    return (widened * scale * gain).astype(jnp.bfloat16)


def shards(
    hidden,
    labels,
    lengths,
    owners,
    w_inner,
    w_bcdt,
    conv_inner,
    conv_bc,
    dt_bias,
    decay_rate,
    d_skip,
    norm_gain,
    w_out,
    final_gain,
    w_head,
):
    rows_own = hidden[0]
    rows_count = rows_own.shape[0]
    blk_count = lax.axis_size("bz") * lax.axis_size("by") * lax.axis_size("bc")
    blk_index = (
        lax.axis_index("bz") * lax.axis_size("by") + lax.axis_index("by")
    ) * lax.axis_size("bc") + lax.axis_index("bc")
    gathered = gather_rows(rows_own)
    tokens_all = gathered.shape[0]
    channels = w_inner.shape[2]
    inner_total = channels * blk_count
    inner_proj = jnp.dot(
        gathered, w_inner.reshape(D, 2 * channels), preferred_element_type=jnp.float32
    ).astype(jnp.bfloat16)
    state_proj = jnp.dot(gathered, w_bcdt, preferred_element_type=jnp.float32).astype(jnp.bfloat16)
    gate_half = inner_proj[:, :channels].astype(jnp.float32)
    segment, position = segments_of(lengths[0], tokens_all)
    conv_value = jax.nn.silu(
        causal_conv(inner_proj[:, channels:].astype(jnp.float32), conv_inner, position)
    )
    conv_state = jax.nn.silu(
        causal_conv(state_proj[:, : 2 * NSTATE].astype(jnp.float32), conv_bc, position)
    )
    input_map = conv_state[:, :NSTATE]
    output_map = conv_state[:, NSTATE:]
    step_size = jax.nn.softplus(state_proj[:, 2 * NSTATE :].astype(jnp.float32) + dt_bias)
    log_heads = -(step_size * decay_rate)
    first_channel = blk_index * channels
    channel_head = (first_channel + jnp.arange(channels, dtype=jnp.int32)) // HEADDIM
    head_low = first_channel // HEADDIM
    head_high = (first_channel + channels - 1) // HEADDIM
    mask_high = (channel_head == head_high).astype(jnp.float32)
    mask_low = 1.0 - mask_high
    step_pair = jnp.concatenate(
        [
            lax.dynamic_slice_in_dim(step_size, head_low, 1, 1),
            lax.dynamic_slice_in_dim(step_size, head_high, 1, 1),
        ],
        axis=1,
    )
    log_pair = jnp.concatenate(
        [
            lax.dynamic_slice_in_dim(log_heads, head_low, 1, 1),
            lax.dynamic_slice_in_dim(log_heads, head_high, 1, 1),
        ],
        axis=1,
    )
    step_channel = step_pair[:, 0:1] * mask_low + step_pair[:, 1:2] * mask_high
    driven = conv_value * step_channel
    slot_masks = (mask_low, mask_high)
    blocks = tokens_all // SCAN_BLOCK
    order = jnp.arange(SCAN_BLOCK, dtype=jnp.int32)
    causal = order[:, None] >= order[None, :]

    def block_step(carry, inputs):
        carried, previous = carry
        drive_block, in_block, out_block, log_block, seg_block = inputs
        cumulative = jnp.cumsum(log_block, axis=0)
        gram = jnp.dot(out_block, in_block.T, precision=HIGH)
        same = (seg_block[:, None] == seg_block[None, :]) & causal
        result = jnp.zeros((SCAN_BLOCK, channels), jnp.float32)
        for slot_index in range(2):
            column = cumulative[:, slot_index]
            spread = jnp.minimum(column[:, None] - column[None, :], 0.0)
            weights = jnp.where(same, jnp.exp(spread), 0.0)
            result = result + jnp.dot(
                gram * weights, drive_block * slot_masks[slot_index], precision=HIGH
            )
        carried_in = carried * (seg_block[0] == previous).astype(jnp.float32)
        rising = jnp.exp(cumulative[:, 0:1]) * mask_low + jnp.exp(cumulative[:, 1:2]) * mask_high
        leading = (seg_block == seg_block[0]).astype(jnp.float32)[:, None]
        result = result + leading * rising * jnp.dot(out_block, carried_in.T, precision=HIGH)
        trailing = (seg_block == seg_block[-1]).astype(jnp.float32)[:, None]
        tail_low = jnp.exp(cumulative[-1:, 0:1] - cumulative[:, 0:1])
        tail_high = jnp.exp(cumulative[-1:, 1:2] - cumulative[:, 1:2])
        tail = tail_low * mask_low + tail_high * mask_high
        whole_block = (seg_block[-1] == seg_block[0]).astype(jnp.float32)
        carried_new = whole_block * rising[-1][:, None] * carried_in + jnp.dot(
            (drive_block * tail * trailing).T, in_block, precision=HIGH
        )
        return ((carried_new, seg_block[-1]), result)

    initial = (jnp.zeros((channels, NSTATE), jnp.float32), jnp.int32(-1))
    scan_inputs = (
        driven.reshape(blocks, SCAN_BLOCK, channels),
        input_map.reshape(blocks, SCAN_BLOCK, NSTATE),
        output_map.reshape(blocks, SCAN_BLOCK, NSTATE),
        log_pair.reshape(blocks, SCAN_BLOCK, 2),
        segment.reshape(blocks, SCAN_BLOCK),
    )
    final_carry, scanned = lax.scan(block_step, initial, scan_inputs)
    mixed = scanned.reshape(tokens_all, channels) + jnp.take(d_skip, channel_head) * conv_value
    gated = mixed * jax.nn.silu(gate_half)
    squares = jnp.sum(gated * gated, axis=1)
    gained = (gated * norm_gain).astype(jnp.bfloat16)
    square_high = squares.astype(jnp.bfloat16)
    square_low = (squares - square_high.astype(jnp.float32)).astype(jnp.bfloat16)
    sent = jnp.concatenate([gained, square_high[:, None], square_low[:, None]], axis=1)
    bz = lax.axis_size("bz")
    by = lax.axis_size("by")
    bc = lax.axis_size("bc")
    sent = sent.reshape(bz, by, bc, rows_count, channels + 2)
    both = lax.all_gather(sent, "bc", axis=0)
    mine = lax.dynamic_index_in_dim(both, lax.axis_index("bc"), axis=3, keepdims=False)
    mine = jnp.transpose(mine, (2, 1, 3, 0, 4))
    half_rows = bz * by * rows_count
    gained_pair = mine[..., :channels].reshape(half_rows, bc * channels)
    squares_pair = jnp.sum(mine[..., channels:].astype(jnp.float32), axis=(3, 4)).reshape(half_rows)
    w_pair = lax.all_gather(w_out, "bc", axis=0, tiled=True)
    partial = jnp.dot(gained_pair, w_pair, preferred_element_type=jnp.float32)
    packed = jnp.concatenate(
        [partial, squares_pair[:, None], jnp.zeros((half_rows, 127), jnp.float32)], axis=1
    )
    packed = packed.reshape(by, bz, rows_count, D + 128)
    packed = lax.psum_scatter(packed, "by", scatter_dimension=0)
    packed_own = lax.psum_scatter(packed, "bz", scatter_dimension=0)
    inverse = lax.rsqrt(packed_own[:, D] / inner_total + EPSILON)
    delta_own = packed_own[:, :D] * inverse[:, None]
    layer_own = (rows_own.astype(jnp.float32) + delta_own).astype(jnp.bfloat16)
    logits = jnp.dot(
        gather_rows(final_norm(layer_own, final_gain)),
        w_head,
        preferred_element_type=jnp.float32,
    )
    vocab_local = w_head.shape[1]
    local_label = labels[0] - blk_index * vocab_local
    hit = jnp.arange(vocab_local, dtype=jnp.int32)[None, :] == local_label[:, None]
    target_local = jnp.sum(jnp.where(hit, logits, 0.0), axis=1)
    top_local = jnp.max(logits, axis=1)
    expsum_local = jnp.sum(jnp.exp(logits - top_local[:, None]), axis=1)
    top_all, expsum_all, target_all = combine_blk(top_local, expsum_local, target_local)
    logprob = target_all - (top_all + jnp.log(expsum_all))
    token_own = lax.dynamic_slice_in_dim(logprob, blk_index * rows_count, rows_count, 0)
    seqs_count = lengths.shape[1]
    onehot = (segment[:, None] == jnp.arange(seqs_count, dtype=jnp.int32)[None, :]).astype(
        jnp.float32
    )
    sums = jnp.dot(logprob, onehot, precision=HIGH)
    seq_index = lax.axis_index("seq")
    mine = lax.dynamic_slice_in_dim(owners, seq_index * seqs_count, seqs_count, 0)
    placement = (mine[:, None] == jnp.arange(owners.shape[0], dtype=jnp.int32)[None, :]).astype(
        jnp.float32
    )
    spread_sums = jnp.dot(sums, placement, precision=HIGH)
    seq_own = lax.psum_scatter(spread_sums, "seq", scatter_dimension=0, tiled=True)
    return (layer_own[None], token_own[None], seq_own)


def solution(mesh):
    blk = mesh.shape["blk"]
    split = mesh.devices.reshape((blk // 16, 8, 2) + mesh.devices.shape[1:])
    mesh = Mesh(split, BLK + mesh.axis_names[1:])
    in_specs = (
        P(("mp", "seq"), BLK, None),
        P("seq", None),
        P("seq", None),
        P(),
        P("mp", None, BLK),
        P("mp", None),
        P("mp", BLK),
        P("mp", None),
        P("mp"),
        P("mp"),
        P("mp"),
        P(("mp",) + BLK),
        P(("mp",) + BLK, None),
        P("mp"),
        P("mp", BLK),
    )
    out_specs = (P(("mp", "seq"), BLK, None), P(("mp", "seq"), BLK), P(("mp", "seq")))
    return jax.shard_map(shards, mesh=mesh, in_specs=in_specs, out_specs=out_specs, check_vma=False)
```

```python
import jax
import jax.numpy as jnp
from jax import lax
from jax.sharding import Mesh
from jax.sharding import PartitionSpec as P

D = 1536
HEADDIM = 64
NSTATE = 128
SCAN_BLOCK = 512
CONV = 4


EPSILON = 1e-05
HIGH = lax.Precision.HIGHEST
BLK = ("bz", "by", "bc")


def gather_rows(rows):
    part = lax.all_gather(rows, "bz", axis=0)
    part = lax.all_gather(part, ("by", "bc"), axis=1)
    return part.reshape((-1,) + rows.shape[1:])


def scatter_rows(values):
    bz = lax.axis_size("bz")
    by = lax.axis_size("by")
    bc = lax.axis_size("bc")
    part = values.reshape((bz, by, bc, -1) + values.shape[1:])
    part = lax.psum_scatter(part, "bc", scatter_dimension=2)
    part = lax.psum_scatter(part, "by", scatter_dimension=1)
    return lax.psum_scatter(part, "bz", scatter_dimension=0)


def sum_blk(values):
    return lax.psum(lax.psum(lax.psum(values, "bc"), "by"), "bz")


def combine_blk(top, expsum, target):
    for axis in ("bc", "by", "bz"):
        pieces = lax.all_gather(jnp.stack([top, expsum, target]), axis, axis=0)
        top = jnp.max(pieces[:, 0], axis=0)
        expsum = jnp.sum(pieces[:, 1] * jnp.exp(pieces[:, 0] - top[None]), axis=0)
        target = jnp.sum(pieces[:, 2], axis=0)
    return top, expsum, target


def segments_of(lengths, count):
    starts = jnp.cumsum(lengths, axis=-1) - lengths
    places = jnp.arange(count, dtype=jnp.int32)
    segment = jnp.sum((places[:, None] >= starts[None, :]).astype(jnp.int32), axis=-1) - 1
    first = jnp.take(starts, segment)
    return (segment, places - first)


def causal_conv(values, weights, position):
    total = values * weights[0]
    for shift_by in range(1, CONV):
        moved = jnp.concatenate(
            [jnp.zeros_like(values[:shift_by, :]), values[:-shift_by, :]], axis=0
        )
        total = (
            total + moved * weights[shift_by] * (position >= shift_by).astype(jnp.float32)[:, None]
        )
    return total


def final_norm(values, gain):
    widened = values.astype(jnp.float32)
    scale = lax.rsqrt(jnp.mean(widened * widened, axis=-1, keepdims=True) + EPSILON)
    return (widened * scale * gain).astype(jnp.bfloat16)


def shards(
    hidden,
    labels,
    lengths,
    owners,
    w_inner,
    w_bcdt,
    conv_inner,
    conv_bc,
    dt_bias,
    decay_rate,
    d_skip,
    norm_gain,
    w_out,
    final_gain,
    w_head,
):
    rows_own = hidden[0]
    rows_count = rows_own.shape[0]
    blk_count = lax.axis_size("bz") * lax.axis_size("by") * lax.axis_size("bc")
    blk_index = (
        lax.axis_index("bz") * lax.axis_size("by") + lax.axis_index("by")
    ) * lax.axis_size("bc") + lax.axis_index("bc")
    gathered = gather_rows(rows_own)
    tokens_all = gathered.shape[0]
    channels = w_inner.shape[2]
    inner_total = channels * blk_count
    inner_proj = jnp.dot(
        gathered, w_inner.reshape(D, 2 * channels), preferred_element_type=jnp.float32
    ).astype(jnp.bfloat16)
    state_proj = jnp.dot(gathered, w_bcdt, preferred_element_type=jnp.float32).astype(jnp.bfloat16)
    gate_half = inner_proj[:, :channels].astype(jnp.float32)
    segment, position = segments_of(lengths[0], tokens_all)
    conv_value = jax.nn.silu(
        causal_conv(inner_proj[:, channels:].astype(jnp.float32), conv_inner, position)
    )
    conv_state = jax.nn.silu(
        causal_conv(state_proj[:, : 2 * NSTATE].astype(jnp.float32), conv_bc, position)
    )
    input_map = conv_state[:, :NSTATE]
    output_map = conv_state[:, NSTATE:]
    step_size = jax.nn.softplus(state_proj[:, 2 * NSTATE :].astype(jnp.float32) + dt_bias)
    log_heads = -(step_size * decay_rate)
    first_channel = blk_index * channels
    channel_head = (first_channel + jnp.arange(channels, dtype=jnp.int32)) // HEADDIM
    head_low = first_channel // HEADDIM
    head_high = (first_channel + channels - 1) // HEADDIM
    mask_high = (channel_head == head_high).astype(jnp.float32)
    mask_low = 1.0 - mask_high
    step_pair = jnp.concatenate(
        [
            lax.dynamic_slice_in_dim(step_size, head_low, 1, 1),
            lax.dynamic_slice_in_dim(step_size, head_high, 1, 1),
        ],
        axis=1,
    )
    log_pair = jnp.concatenate(
        [
            lax.dynamic_slice_in_dim(log_heads, head_low, 1, 1),
            lax.dynamic_slice_in_dim(log_heads, head_high, 1, 1),
        ],
        axis=1,
    )
    step_channel = step_pair[:, 0:1] * mask_low + step_pair[:, 1:2] * mask_high
    driven = conv_value * step_channel
    slot_masks = (mask_low, mask_high)
    blocks = tokens_all // SCAN_BLOCK
    order = jnp.arange(SCAN_BLOCK, dtype=jnp.int32)
    causal = order[:, None] >= order[None, :]

    def block_step(carry, inputs):
        carried, previous = carry
        drive_block, in_block, out_block, log_block, seg_block = inputs
        cumulative = jnp.cumsum(log_block, axis=0)
        gram = jnp.dot(out_block, in_block.T, precision=HIGH)
        same = (seg_block[:, None] == seg_block[None, :]) & causal
        result = jnp.zeros((SCAN_BLOCK, channels), jnp.float32)
        for slot_index in range(2):
            column = cumulative[:, slot_index]
            spread = jnp.minimum(column[:, None] - column[None, :], 0.0)
            weights = jnp.where(same, jnp.exp(spread), 0.0)
            result = result + jnp.dot(
                gram * weights, drive_block * slot_masks[slot_index], precision=HIGH
            )
        carried_in = carried * (seg_block[0] == previous).astype(jnp.float32)
        rising = jnp.exp(cumulative[:, 0:1]) * mask_low + jnp.exp(cumulative[:, 1:2]) * mask_high
        leading = (seg_block == seg_block[0]).astype(jnp.float32)[:, None]
        result = result + leading * rising * jnp.dot(out_block, carried_in.T, precision=HIGH)
        trailing = (seg_block == seg_block[-1]).astype(jnp.float32)[:, None]
        tail_low = jnp.exp(cumulative[-1:, 0:1] - cumulative[:, 0:1])
        tail_high = jnp.exp(cumulative[-1:, 1:2] - cumulative[:, 1:2])
        tail = tail_low * mask_low + tail_high * mask_high
        whole_block = (seg_block[-1] == seg_block[0]).astype(jnp.float32)
        carried_new = whole_block * rising[-1][:, None] * carried_in + jnp.dot(
            (drive_block * tail * trailing).T, in_block, precision=HIGH
        )
        return ((carried_new, seg_block[-1]), result)

    initial = (jnp.zeros((channels, NSTATE), jnp.float32), jnp.int32(-1))
    scan_inputs = (
        driven.reshape(blocks, SCAN_BLOCK, channels),
        input_map.reshape(blocks, SCAN_BLOCK, NSTATE),
        output_map.reshape(blocks, SCAN_BLOCK, NSTATE),
        log_pair.reshape(blocks, SCAN_BLOCK, 2),
        segment.reshape(blocks, SCAN_BLOCK),
    )
    final_carry, scanned = lax.scan(block_step, initial, scan_inputs)
    mixed = scanned.reshape(tokens_all, channels) + jnp.take(d_skip, channel_head) * conv_value
    gated = mixed * jax.nn.silu(gate_half)
    squares = jnp.sum(gated * gated, axis=1)
    gained = (gated * norm_gain).astype(jnp.bfloat16)
    square_high = squares.astype(jnp.bfloat16)
    square_low = (squares - square_high.astype(jnp.float32)).astype(jnp.bfloat16)
    sent = jnp.concatenate([gained, square_high[:, None], square_low[:, None]], axis=1)
    bz = lax.axis_size("bz")
    by = lax.axis_size("by")
    bc = lax.axis_size("bc")
    sent = sent.reshape(bz, by, bc, rows_count, channels + 2)
    both = lax.all_gather(sent, "bc", axis=0)
    mine = lax.dynamic_index_in_dim(both, lax.axis_index("bc"), axis=3, keepdims=False)
    mine = jnp.transpose(mine, (2, 1, 3, 0, 4))
    half_rows = bz * by * rows_count
    gained_pair = mine[..., :channels].reshape(half_rows, bc * channels)
    squares_pair = jnp.sum(mine[..., channels:].astype(jnp.float32), axis=(3, 4)).reshape(half_rows)
    w_pair = lax.all_gather(w_out, "bc", axis=0, tiled=True)
    partial = jnp.dot(gained_pair, w_pair, preferred_element_type=jnp.float32)
    packed = jnp.concatenate(
        [partial, squares_pair[:, None], jnp.zeros((half_rows, 127), jnp.float32)], axis=1
    )
    packed = packed.reshape(by, bz, rows_count, D + 128)
    packed = lax.psum_scatter(packed, "by", scatter_dimension=0)
    packed_own = lax.psum_scatter(packed, "bz", scatter_dimension=0)
    inverse = lax.rsqrt(packed_own[:, D] / inner_total + EPSILON)
    delta_own = packed_own[:, :D] * inverse[:, None]
    layer_own = (rows_own.astype(jnp.float32) + delta_own).astype(jnp.bfloat16)
    logits = jnp.dot(
        gather_rows(final_norm(layer_own, final_gain)),
        w_head,
        preferred_element_type=jnp.float32,
    )
    vocab_local = w_head.shape[1]
    local_label = labels[0] - blk_index * vocab_local
    hit = jnp.arange(vocab_local, dtype=jnp.int32)[None, :] == local_label[:, None]
    target_local = jnp.sum(jnp.where(hit, logits, 0.0), axis=1)
    top_local = jnp.max(logits, axis=1)
    expsum_local = jnp.sum(jnp.exp(logits - top_local[:, None]), axis=1)
    top_all, expsum_all, target_all = combine_blk(top_local, expsum_local, target_local)
    logprob = target_all - (top_all + jnp.log(expsum_all))
    token_own = lax.dynamic_slice_in_dim(logprob, blk_index * rows_count, rows_count, 0)
    seqs_count = lengths.shape[1]
    onehot = (segment[:, None] == jnp.arange(seqs_count, dtype=jnp.int32)[None, :]).astype(
        jnp.float32
    )
    sums = jnp.dot(logprob, onehot, precision=HIGH)
    seq_index = lax.axis_index("seq")
    mine = lax.dynamic_slice_in_dim(owners, seq_index * seqs_count, seqs_count, 0)
    placement = (mine[:, None] == jnp.arange(owners.shape[0], dtype=jnp.int32)[None, :]).astype(
        jnp.float32
    )
    spread_sums = jnp.dot(sums, placement, precision=HIGH)
    seq_own = lax.psum_scatter(spread_sums, "seq", scatter_dimension=0, tiled=True)
    return (layer_own[None], token_own[None], seq_own)


def solution(mesh):
    blk = mesh.shape["blk"]
    split = mesh.devices.reshape((blk // 16, 8, 2) + mesh.devices.shape[1:])
    mesh = Mesh(split, BLK + mesh.axis_names[1:])
    in_specs = (
        P(("mp", "seq"), BLK, None),
        P("seq", None),
        P("seq", None),
        P(),
        P("mp", None, BLK),
        P("mp", None),
        P("mp", BLK),
        P("mp", None),
        P("mp"),
        P("mp"),
        P("mp"),
        P(("mp",) + BLK),
        P(("mp",) + BLK, None),
        P("mp"),
        P("mp", BLK),
    )
    out_specs = (P(("mp", "seq"), BLK, None), P(("mp", "seq"), BLK), P(("mp", "seq")))
    return jax.shard_map(shards, mesh=mesh, in_specs=in_specs, out_specs=out_specs, check_vma=False)
```

```python
import jax
import jax.numpy as jnp
from jax import lax
from jax.sharding import Mesh
from jax.sharding import PartitionSpec as P

D = 1536
HEADDIM = 64
NSTATE = 128
SCAN_BLOCK = 512
CONV = 4


EPSILON = 1e-05
HIGH = lax.Precision.HIGHEST
BLK = ("bz", "by", "bc")


def gather_rows(rows):
    part = lax.all_gather(rows, "bz", axis=0)
    part = lax.all_gather(part, ("by", "bc"), axis=1)
    return part.reshape((-1,) + rows.shape[1:])


def scatter_rows(values):
    bz = lax.axis_size("bz")
    by = lax.axis_size("by")
    bc = lax.axis_size("bc")
    part = values.reshape((bz, by, bc, -1) + values.shape[1:])
    part = lax.psum_scatter(part, "bc", scatter_dimension=2)
    part = lax.psum_scatter(part, "by", scatter_dimension=1)
    return lax.psum_scatter(part, "bz", scatter_dimension=0)


def sum_blk(values):
    return lax.psum(lax.psum(lax.psum(values, "bc"), "by"), "bz")


def combine_blk(top, expsum, target):
    for axis in ("bc", "by", "bz"):
        pieces = lax.all_gather(jnp.stack([top, expsum, target]), axis, axis=0)
        top = jnp.max(pieces[:, 0], axis=0)
        expsum = jnp.sum(pieces[:, 1] * jnp.exp(pieces[:, 0] - top[None]), axis=0)
        target = jnp.sum(pieces[:, 2], axis=0)
    return top, expsum, target


def segments_of(lengths, count):
    starts = jnp.cumsum(lengths, axis=-1) - lengths
    places = jnp.arange(count, dtype=jnp.int32)
    segment = jnp.sum((places[:, None] >= starts[None, :]).astype(jnp.int32), axis=-1) - 1
    first = jnp.take(starts, segment)
    return (segment, places - first)


def causal_conv(values, weights, position):
    total = values * weights[0]
    for shift_by in range(1, CONV):
        moved = jnp.concatenate(
            [jnp.zeros_like(values[:shift_by, :]), values[:-shift_by, :]], axis=0
        )
        total = (
            total + moved * weights[shift_by] * (position >= shift_by).astype(jnp.float32)[:, None]
        )
    return total


def final_norm(values, gain):
    widened = values.astype(jnp.float32)
    scale = lax.rsqrt(jnp.mean(widened * widened, axis=-1, keepdims=True) + EPSILON)
    return (widened * scale * gain).astype(jnp.bfloat16)


def shards(
    hidden,
    labels,
    lengths,
    owners,
    w_inner,
    w_bcdt,
    conv_inner,
    conv_bc,
    dt_bias,
    decay_rate,
    d_skip,
    norm_gain,
    w_out,
    final_gain,
    w_head,
):
    rows_own = hidden[0]
    rows_count = rows_own.shape[0]
    blk_count = lax.axis_size("bz") * lax.axis_size("by") * lax.axis_size("bc")
    blk_index = (
        lax.axis_index("bz") * lax.axis_size("by") + lax.axis_index("by")
    ) * lax.axis_size("bc") + lax.axis_index("bc")
    gathered = gather_rows(rows_own)
    tokens_all = gathered.shape[0]
    channels = w_inner.shape[2]
    inner_total = channels * blk_count
    inner_proj = jnp.dot(
        gathered, w_inner.reshape(D, 2 * channels), preferred_element_type=jnp.float32
    ).astype(jnp.bfloat16)
    state_proj = jnp.dot(gathered, w_bcdt, preferred_element_type=jnp.float32).astype(jnp.bfloat16)
    gate_half = inner_proj[:, :channels].astype(jnp.float32)
    segment, position = segments_of(lengths[0], tokens_all)
    conv_value = jax.nn.silu(
        causal_conv(inner_proj[:, channels:].astype(jnp.float32), conv_inner, position)
    )
    conv_state = jax.nn.silu(
        causal_conv(state_proj[:, : 2 * NSTATE].astype(jnp.float32), conv_bc, position)
    )
    input_map = conv_state[:, :NSTATE]
    output_map = conv_state[:, NSTATE:]
    step_size = jax.nn.softplus(state_proj[:, 2 * NSTATE :].astype(jnp.float32) + dt_bias)
    log_heads = -(step_size * decay_rate)
    first_channel = blk_index * channels
    channel_head = (first_channel + jnp.arange(channels, dtype=jnp.int32)) // HEADDIM
    head_low = first_channel // HEADDIM
    head_high = (first_channel + channels - 1) // HEADDIM
    mask_high = (channel_head == head_high).astype(jnp.float32)
    mask_low = 1.0 - mask_high
    step_pair = jnp.concatenate(
        [
            lax.dynamic_slice_in_dim(step_size, head_low, 1, 1),
            lax.dynamic_slice_in_dim(step_size, head_high, 1, 1),
        ],
        axis=1,
    )
    log_pair = jnp.concatenate(
        [
            lax.dynamic_slice_in_dim(log_heads, head_low, 1, 1),
            lax.dynamic_slice_in_dim(log_heads, head_high, 1, 1),
        ],
        axis=1,
    )
    step_channel = step_pair[:, 0:1] * mask_low + step_pair[:, 1:2] * mask_high
    driven = conv_value * step_channel
    slot_masks = (mask_low, mask_high)
    blocks = tokens_all // SCAN_BLOCK
    order = jnp.arange(SCAN_BLOCK, dtype=jnp.int32)
    causal = order[:, None] >= order[None, :]

    def block_step(carry, inputs):
        carried, previous = carry
        drive_block, in_block, out_block, log_block, seg_block = inputs
        cumulative = jnp.cumsum(log_block, axis=0)
        gram = jnp.dot(out_block, in_block.T, precision=HIGH)
        same = (seg_block[:, None] == seg_block[None, :]) & causal
        result = jnp.zeros((SCAN_BLOCK, channels), jnp.float32)
        for slot_index in range(2):
            column = cumulative[:, slot_index]
            spread = jnp.minimum(column[:, None] - column[None, :], 0.0)
            weights = jnp.where(same, jnp.exp(spread), 0.0)
            result = result + jnp.dot(
                gram * weights, drive_block * slot_masks[slot_index], precision=HIGH
            )
        carried_in = carried * (seg_block[0] == previous).astype(jnp.float32)
        rising = jnp.exp(cumulative[:, 0:1]) * mask_low + jnp.exp(cumulative[:, 1:2]) * mask_high
        leading = (seg_block == seg_block[0]).astype(jnp.float32)[:, None]
        result = result + leading * rising * jnp.dot(out_block, carried_in.T, precision=HIGH)
        trailing = (seg_block == seg_block[-1]).astype(jnp.float32)[:, None]
        tail_low = jnp.exp(cumulative[-1:, 0:1] - cumulative[:, 0:1])
        tail_high = jnp.exp(cumulative[-1:, 1:2] - cumulative[:, 1:2])
        tail = tail_low * mask_low + tail_high * mask_high
        whole_block = (seg_block[-1] == seg_block[0]).astype(jnp.float32)
        carried_new = whole_block * rising[-1][:, None] * carried_in + jnp.dot(
            (drive_block * tail * trailing).T, in_block, precision=HIGH
        )
        return ((carried_new, seg_block[-1]), result)

    initial = (jnp.zeros((channels, NSTATE), jnp.float32), jnp.int32(-1))
    scan_inputs = (
        driven.reshape(blocks, SCAN_BLOCK, channels),
        input_map.reshape(blocks, SCAN_BLOCK, NSTATE),
        output_map.reshape(blocks, SCAN_BLOCK, NSTATE),
        log_pair.reshape(blocks, SCAN_BLOCK, 2),
        segment.reshape(blocks, SCAN_BLOCK),
    )
    final_carry, scanned = lax.scan(block_step, initial, scan_inputs)
    mixed = scanned.reshape(tokens_all, channels) + jnp.take(d_skip, channel_head) * conv_value
    gated = mixed * jax.nn.silu(gate_half)
    squares = jnp.sum(gated * gated, axis=1)
    gained = (gated * norm_gain).astype(jnp.bfloat16)
    square_high = squares.astype(jnp.bfloat16)
    square_low = (squares - square_high.astype(jnp.float32)).astype(jnp.bfloat16)
    sent = jnp.concatenate([gained, square_high[:, None], square_low[:, None]], axis=1)
    bz = lax.axis_size("bz")
    by = lax.axis_size("by")
    bc = lax.axis_size("bc")
    sent = sent.reshape(bz, by, bc, rows_count, channels + 2)
    both = lax.all_gather(sent, "bc", axis=0)
    mine = lax.dynamic_index_in_dim(both, lax.axis_index("bc"), axis=3, keepdims=False)
    mine = jnp.transpose(mine, (2, 1, 3, 0, 4))
    half_rows = bz * by * rows_count
    gained_pair = mine[..., :channels].reshape(half_rows, bc * channels)
    squares_pair = jnp.sum(mine[..., channels:].astype(jnp.float32), axis=(3, 4)).reshape(half_rows)
    w_pair = lax.all_gather(w_out, "bc", axis=0, tiled=True)
    partial = jnp.dot(gained_pair, w_pair, preferred_element_type=jnp.float32)
    packed = jnp.concatenate(
        [partial, squares_pair[:, None], jnp.zeros((half_rows, 127), jnp.float32)], axis=1
    )
    packed = packed.reshape(by, bz, rows_count, D + 128).astype(jnp.bfloat16)
    packed = lax.psum_scatter(packed, "by", scatter_dimension=0).astype(jnp.float32)
    packed_own = lax.psum_scatter(packed, "bz", scatter_dimension=0)
    inverse = lax.rsqrt(packed_own[:, D] / inner_total + EPSILON)
    delta_own = packed_own[:, :D] * inverse[:, None]
    layer_own = (rows_own.astype(jnp.float32) + delta_own).astype(jnp.bfloat16)
    logits = jnp.dot(
        gather_rows(final_norm(layer_own, final_gain)),
        w_head,
        preferred_element_type=jnp.float32,
    )
    vocab_local = w_head.shape[1]
    local_label = labels[0] - blk_index * vocab_local
    hit = jnp.arange(vocab_local, dtype=jnp.int32)[None, :] == local_label[:, None]
    target_local = jnp.sum(jnp.where(hit, logits, 0.0), axis=1)
    top_local = jnp.max(logits, axis=1)
    expsum_local = jnp.sum(jnp.exp(logits - top_local[:, None]), axis=1)
    top_all, expsum_all, target_all = combine_blk(top_local, expsum_local, target_local)
    logprob = target_all - (top_all + jnp.log(expsum_all))
    token_own = lax.dynamic_slice_in_dim(logprob, blk_index * rows_count, rows_count, 0)
    seqs_count = lengths.shape[1]
    onehot = (segment[:, None] == jnp.arange(seqs_count, dtype=jnp.int32)[None, :]).astype(
        jnp.float32
    )
    sums = jnp.dot(logprob, onehot, precision=HIGH)
    seq_index = lax.axis_index("seq")
    mine = lax.dynamic_slice_in_dim(owners, seq_index * seqs_count, seqs_count, 0)
    placement = (mine[:, None] == jnp.arange(owners.shape[0], dtype=jnp.int32)[None, :]).astype(
        jnp.float32
    )
    spread_sums = jnp.dot(sums, placement, precision=HIGH)
    seq_own = lax.psum_scatter(spread_sums, "seq", scatter_dimension=0, tiled=True)
    return (layer_own[None], token_own[None], seq_own)


def solution(mesh):
    blk = mesh.shape["blk"]
    split = mesh.devices.reshape((blk // 16, 8, 2) + mesh.devices.shape[1:])
    mesh = Mesh(split, BLK + mesh.axis_names[1:])
    in_specs = (
        P(("mp", "seq"), BLK, None),
        P("seq", None),
        P("seq", None),
        P(),
        P("mp", None, BLK),
        P("mp", None),
        P("mp", BLK),
        P("mp", None),
        P("mp"),
        P("mp"),
        P("mp"),
        P(("mp",) + BLK),
        P(("mp",) + BLK, None),
        P("mp"),
        P("mp", BLK),
    )
    out_specs = (P(("mp", "seq"), BLK, None), P(("mp", "seq"), BLK), P(("mp", "seq")))
    return jax.shard_map(shards, mesh=mesh, in_specs=in_specs, out_specs=out_specs, check_vma=False)
```

```python
import jax
import jax.numpy as jnp
from jax import lax
from jax.sharding import Mesh
from jax.sharding import PartitionSpec as P

D = 1536
HEADDIM = 64
NSTATE = 128
SCAN_BLOCK = 512
CONV = 4


EPSILON = 1e-05
HIGH = lax.Precision.HIGHEST
BLK = ("bz", "by", "bc")


def gather_rows(rows):
    part = lax.all_gather(rows, "bz", axis=0)
    part = lax.all_gather(part, ("by", "bc"), axis=1)
    return part.reshape((-1,) + rows.shape[1:])


def scatter_rows(values):
    bz = lax.axis_size("bz")
    by = lax.axis_size("by")
    bc = lax.axis_size("bc")
    part = values.reshape((bz, by, bc, -1) + values.shape[1:])
    part = lax.psum_scatter(part, "bc", scatter_dimension=2)
    part = lax.psum_scatter(part, "by", scatter_dimension=1)
    return lax.psum_scatter(part, "bz", scatter_dimension=0)


def sum_blk(values):
    return lax.psum(lax.psum(lax.psum(values, "bc"), "by"), "bz")


def combine_blk(top, expsum, target):
    for axis in (("by", "bc"), "bz"):
        pieces = lax.all_gather(jnp.stack([top, expsum, target]), axis, axis=0)
        top = jnp.max(pieces[:, 0], axis=0)
        expsum = jnp.sum(pieces[:, 1] * jnp.exp(pieces[:, 0] - top[None]), axis=0)
        target = jnp.sum(pieces[:, 2], axis=0)
    return top, expsum, target


def segments_of(lengths, count):
    starts = jnp.cumsum(lengths, axis=-1) - lengths
    places = jnp.arange(count, dtype=jnp.int32)
    segment = jnp.sum((places[:, None] >= starts[None, :]).astype(jnp.int32), axis=-1) - 1
    first = jnp.take(starts, segment)
    return (segment, places - first)


def causal_conv(values, weights, position):
    total = values * weights[0]
    for shift_by in range(1, CONV):
        moved = jnp.concatenate(
            [jnp.zeros_like(values[:shift_by, :]), values[:-shift_by, :]], axis=0
        )
        total = (
            total + moved * weights[shift_by] * (position >= shift_by).astype(jnp.float32)[:, None]
        )
    return total


def final_norm(values, gain):
    widened = values.astype(jnp.float32)
    scale = lax.rsqrt(jnp.mean(widened * widened, axis=-1, keepdims=True) + EPSILON)
    return (widened * scale * gain).astype(jnp.bfloat16)


def shards(
    hidden,
    labels,
    lengths,
    owners,
    w_inner,
    w_bcdt,
    conv_inner,
    conv_bc,
    dt_bias,
    decay_rate,
    d_skip,
    norm_gain,
    w_out,
    final_gain,
    w_head,
):
    rows_own = hidden[0]
    rows_count = rows_own.shape[0]
    blk_count = lax.axis_size("bz") * lax.axis_size("by") * lax.axis_size("bc")
    blk_index = (
        lax.axis_index("bz") * lax.axis_size("by") + lax.axis_index("by")
    ) * lax.axis_size("bc") + lax.axis_index("bc")
    gathered = gather_rows(rows_own)
    tokens_all = gathered.shape[0]
    channels = w_inner.shape[2]
    inner_total = channels * blk_count
    inner_proj = jnp.dot(
        gathered, w_inner.reshape(D, 2 * channels), preferred_element_type=jnp.float32
    ).astype(jnp.bfloat16)
    state_proj = jnp.dot(gathered, w_bcdt, preferred_element_type=jnp.float32).astype(jnp.bfloat16)
    gate_half = inner_proj[:, :channels].astype(jnp.float32)
    segment, position = segments_of(lengths[0], tokens_all)
    conv_value = jax.nn.silu(
        causal_conv(inner_proj[:, channels:].astype(jnp.float32), conv_inner, position)
    )
    conv_state = jax.nn.silu(
        causal_conv(state_proj[:, : 2 * NSTATE].astype(jnp.float32), conv_bc, position)
    )
    input_map = conv_state[:, :NSTATE]
    output_map = conv_state[:, NSTATE:]
    step_size = jax.nn.softplus(state_proj[:, 2 * NSTATE :].astype(jnp.float32) + dt_bias)
    log_heads = -(step_size * decay_rate)
    first_channel = blk_index * channels
    channel_head = (first_channel + jnp.arange(channels, dtype=jnp.int32)) // HEADDIM
    head_low = first_channel // HEADDIM
    head_high = (first_channel + channels - 1) // HEADDIM
    mask_high = (channel_head == head_high).astype(jnp.float32)
    mask_low = 1.0 - mask_high
    step_pair = jnp.concatenate(
        [
            lax.dynamic_slice_in_dim(step_size, head_low, 1, 1),
            lax.dynamic_slice_in_dim(step_size, head_high, 1, 1),
        ],
        axis=1,
    )
    log_pair = jnp.concatenate(
        [
            lax.dynamic_slice_in_dim(log_heads, head_low, 1, 1),
            lax.dynamic_slice_in_dim(log_heads, head_high, 1, 1),
        ],
        axis=1,
    )
    step_channel = step_pair[:, 0:1] * mask_low + step_pair[:, 1:2] * mask_high
    driven = conv_value * step_channel
    slot_masks = (mask_low, mask_high)
    blocks = tokens_all // SCAN_BLOCK
    order = jnp.arange(SCAN_BLOCK, dtype=jnp.int32)
    causal = order[:, None] >= order[None, :]

    def block_step(carry, inputs):
        carried, previous = carry
        drive_block, in_block, out_block, log_block, seg_block = inputs
        cumulative = jnp.cumsum(log_block, axis=0)
        gram = jnp.dot(out_block, in_block.T, precision=HIGH)
        same = (seg_block[:, None] == seg_block[None, :]) & causal
        result = jnp.zeros((SCAN_BLOCK, channels), jnp.float32)
        for slot_index in range(2):
            column = cumulative[:, slot_index]
            spread = jnp.minimum(column[:, None] - column[None, :], 0.0)
            weights = jnp.where(same, jnp.exp(spread), 0.0)
            result = result + jnp.dot(
                gram * weights, drive_block * slot_masks[slot_index], precision=HIGH
            )
        carried_in = carried * (seg_block[0] == previous).astype(jnp.float32)
        rising = jnp.exp(cumulative[:, 0:1]) * mask_low + jnp.exp(cumulative[:, 1:2]) * mask_high
        leading = (seg_block == seg_block[0]).astype(jnp.float32)[:, None]
        result = result + leading * rising * jnp.dot(out_block, carried_in.T, precision=HIGH)
        trailing = (seg_block == seg_block[-1]).astype(jnp.float32)[:, None]
        tail_low = jnp.exp(cumulative[-1:, 0:1] - cumulative[:, 0:1])
        tail_high = jnp.exp(cumulative[-1:, 1:2] - cumulative[:, 1:2])
        tail = tail_low * mask_low + tail_high * mask_high
        whole_block = (seg_block[-1] == seg_block[0]).astype(jnp.float32)
        carried_new = whole_block * rising[-1][:, None] * carried_in + jnp.dot(
            (drive_block * tail * trailing).T, in_block, precision=HIGH
        )
        return ((carried_new, seg_block[-1]), result)

    initial = (jnp.zeros((channels, NSTATE), jnp.float32), jnp.int32(-1))
    scan_inputs = (
        driven.reshape(blocks, SCAN_BLOCK, channels),
        input_map.reshape(blocks, SCAN_BLOCK, NSTATE),
        output_map.reshape(blocks, SCAN_BLOCK, NSTATE),
        log_pair.reshape(blocks, SCAN_BLOCK, 2),
        segment.reshape(blocks, SCAN_BLOCK),
    )
    final_carry, scanned = lax.scan(block_step, initial, scan_inputs)
    mixed = scanned.reshape(tokens_all, channels) + jnp.take(d_skip, channel_head) * conv_value
    gated = mixed * jax.nn.silu(gate_half)
    squares = jnp.sum(gated * gated, axis=1)
    gained = (gated * norm_gain).astype(jnp.bfloat16)
    square_high = squares.astype(jnp.bfloat16)
    square_low = (squares - square_high.astype(jnp.float32)).astype(jnp.bfloat16)
    sent = jnp.concatenate([gained, square_high[:, None], square_low[:, None]], axis=1)
    bz = lax.axis_size("bz")
    by = lax.axis_size("by")
    bc = lax.axis_size("bc")
    sent = sent.reshape(bz, by, bc, rows_count, channels + 2)
    both = lax.all_gather(sent, "bc", axis=0)
    mine = lax.dynamic_index_in_dim(both, lax.axis_index("bc"), axis=3, keepdims=False)
    mine = jnp.transpose(mine, (2, 1, 3, 0, 4))
    half_rows = bz * by * rows_count
    gained_pair = mine[..., :channels].reshape(half_rows, bc * channels)
    squares_pair = jnp.sum(mine[..., channels:].astype(jnp.float32), axis=(3, 4)).reshape(half_rows)
    w_pair = lax.all_gather(w_out, "bc", axis=0, tiled=True)
    partial = jnp.dot(gained_pair, w_pair, preferred_element_type=jnp.float32)
    packed = jnp.concatenate(
        [partial, squares_pair[:, None], jnp.zeros((half_rows, 127), jnp.float32)], axis=1
    )
    packed = packed.reshape(by, bz, rows_count, D + 128)
    packed = lax.psum_scatter(packed, "by", scatter_dimension=0)
    packed_own = lax.psum_scatter(packed, "bz", scatter_dimension=0)
    inverse = lax.rsqrt(packed_own[:, D] / inner_total + EPSILON)
    delta_own = packed_own[:, :D] * inverse[:, None]
    layer_own = (rows_own.astype(jnp.float32) + delta_own).astype(jnp.bfloat16)
    logits = jnp.dot(
        gather_rows(final_norm(layer_own, final_gain)),
        w_head,
        preferred_element_type=jnp.float32,
    )
    vocab_local = w_head.shape[1]
    local_label = labels[0] - blk_index * vocab_local
    hit = jnp.arange(vocab_local, dtype=jnp.int32)[None, :] == local_label[:, None]
    target_local = jnp.sum(jnp.where(hit, logits, 0.0), axis=1)
    top_local = jnp.max(logits, axis=1)
    expsum_local = jnp.sum(jnp.exp(logits - top_local[:, None]), axis=1)
    top_all, expsum_all, target_all = combine_blk(top_local, expsum_local, target_local)
    logprob = target_all - (top_all + jnp.log(expsum_all))
    token_own = lax.dynamic_slice_in_dim(logprob, blk_index * rows_count, rows_count, 0)
    seqs_count = lengths.shape[1]
    onehot = (segment[:, None] == jnp.arange(seqs_count, dtype=jnp.int32)[None, :]).astype(
        jnp.float32
    )
    sums = jnp.dot(logprob, onehot, precision=HIGH)
    seq_index = lax.axis_index("seq")
    mine = lax.dynamic_slice_in_dim(owners, seq_index * seqs_count, seqs_count, 0)
    placement = (mine[:, None] == jnp.arange(owners.shape[0], dtype=jnp.int32)[None, :]).astype(
        jnp.float32
    )
    spread_sums = jnp.dot(sums, placement, precision=HIGH)
    seq_own = lax.psum_scatter(spread_sums, "seq", scatter_dimension=0, tiled=True)
    return (layer_own[None], token_own[None], seq_own)


def solution(mesh):
    blk = mesh.shape["blk"]
    split = mesh.devices.reshape((blk // 16, 8, 2) + mesh.devices.shape[1:])
    mesh = Mesh(split, BLK + mesh.axis_names[1:])
    in_specs = (
        P(("mp", "seq"), BLK, None),
        P("seq", None),
        P("seq", None),
        P(),
        P("mp", None, BLK),
        P("mp", None),
        P("mp", BLK),
        P("mp", None),
        P("mp"),
        P("mp"),
        P("mp"),
        P(("mp",) + BLK),
        P(("mp",) + BLK, None),
        P("mp"),
        P("mp", BLK),
    )
    out_specs = (P(("mp", "seq"), BLK, None), P(("mp", "seq"), BLK), P(("mp", "seq")))
    return jax.shard_map(shards, mesh=mesh, in_specs=in_specs, out_specs=out_specs, check_vma=False)
```

```python
import jax
import jax.numpy as jnp
from jax import lax
from jax.sharding import Mesh
from jax.sharding import PartitionSpec as P

D = 1536
HEADDIM = 64
NSTATE = 128
SCAN_BLOCK = 512
CONV = 4


EPSILON = 1e-05
HIGH = lax.Precision.HIGHEST
BLK = ("bz", "by", "bc")


def gather_rows(rows):
    part = lax.all_gather(rows, "bz", axis=0)
    part = lax.all_gather(part, ("by", "bc"), axis=1)
    return part.reshape((-1,) + rows.shape[1:])


def scatter_rows(values):
    bz = lax.axis_size("bz")
    by = lax.axis_size("by")
    bc = lax.axis_size("bc")
    part = values.reshape((bz, by, bc, -1) + values.shape[1:])
    part = lax.psum_scatter(part, "bc", scatter_dimension=2)
    part = lax.psum_scatter(part, "by", scatter_dimension=1)
    return lax.psum_scatter(part, "bz", scatter_dimension=0)


def sum_blk(values):
    return lax.psum(lax.psum(lax.psum(values, "bc"), "by"), "bz")


def combine_blk(top, expsum, target):
    for axis in (("bz", "by", "bc"),):
        pieces = lax.all_gather(jnp.stack([top, expsum, target]), axis, axis=0)
        top = jnp.max(pieces[:, 0], axis=0)
        expsum = jnp.sum(pieces[:, 1] * jnp.exp(pieces[:, 0] - top[None]), axis=0)
        target = jnp.sum(pieces[:, 2], axis=0)
    return top, expsum, target


def segments_of(lengths, count):
    starts = jnp.cumsum(lengths, axis=-1) - lengths
    places = jnp.arange(count, dtype=jnp.int32)
    segment = jnp.sum((places[:, None] >= starts[None, :]).astype(jnp.int32), axis=-1) - 1
    first = jnp.take(starts, segment)
    return (segment, places - first)


def causal_conv(values, weights, position):
    total = values * weights[0]
    for shift_by in range(1, CONV):
        moved = jnp.concatenate(
            [jnp.zeros_like(values[:shift_by, :]), values[:-shift_by, :]], axis=0
        )
        total = (
            total + moved * weights[shift_by] * (position >= shift_by).astype(jnp.float32)[:, None]
        )
    return total


def final_norm(values, gain):
    widened = values.astype(jnp.float32)
    scale = lax.rsqrt(jnp.mean(widened * widened, axis=-1, keepdims=True) + EPSILON)
    return (widened * scale * gain).astype(jnp.bfloat16)


def shards(
    hidden,
    labels,
    lengths,
    owners,
    w_inner,
    w_bcdt,
    conv_inner,
    conv_bc,
    dt_bias,
    decay_rate,
    d_skip,
    norm_gain,
    w_out,
    final_gain,
    w_head,
):
    rows_own = hidden[0]
    rows_count = rows_own.shape[0]
    blk_count = lax.axis_size("bz") * lax.axis_size("by") * lax.axis_size("bc")
    blk_index = (
        lax.axis_index("bz") * lax.axis_size("by") + lax.axis_index("by")
    ) * lax.axis_size("bc") + lax.axis_index("bc")
    gathered = gather_rows(rows_own)
    tokens_all = gathered.shape[0]
    channels = w_inner.shape[2]
    inner_total = channels * blk_count
    inner_proj = jnp.dot(
        gathered, w_inner.reshape(D, 2 * channels), preferred_element_type=jnp.float32
    ).astype(jnp.bfloat16)
    state_proj = jnp.dot(gathered, w_bcdt, preferred_element_type=jnp.float32).astype(jnp.bfloat16)
    gate_half = inner_proj[:, :channels].astype(jnp.float32)
    segment, position = segments_of(lengths[0], tokens_all)
    conv_value = jax.nn.silu(
        causal_conv(inner_proj[:, channels:].astype(jnp.float32), conv_inner, position)
    )
    conv_state = jax.nn.silu(
        causal_conv(state_proj[:, : 2 * NSTATE].astype(jnp.float32), conv_bc, position)
    )
    input_map = conv_state[:, :NSTATE]
    output_map = conv_state[:, NSTATE:]
    step_size = jax.nn.softplus(state_proj[:, 2 * NSTATE :].astype(jnp.float32) + dt_bias)
    log_heads = -(step_size * decay_rate)
    first_channel = blk_index * channels
    channel_head = (first_channel + jnp.arange(channels, dtype=jnp.int32)) // HEADDIM
    head_low = first_channel // HEADDIM
    head_high = (first_channel + channels - 1) // HEADDIM
    mask_high = (channel_head == head_high).astype(jnp.float32)
    mask_low = 1.0 - mask_high
    step_pair = jnp.concatenate(
        [
            lax.dynamic_slice_in_dim(step_size, head_low, 1, 1),
            lax.dynamic_slice_in_dim(step_size, head_high, 1, 1),
        ],
        axis=1,
    )
    log_pair = jnp.concatenate(
        [
            lax.dynamic_slice_in_dim(log_heads, head_low, 1, 1),
            lax.dynamic_slice_in_dim(log_heads, head_high, 1, 1),
        ],
        axis=1,
    )
    step_channel = step_pair[:, 0:1] * mask_low + step_pair[:, 1:2] * mask_high
    driven = conv_value * step_channel
    slot_masks = (mask_low, mask_high)
    blocks = tokens_all // SCAN_BLOCK
    order = jnp.arange(SCAN_BLOCK, dtype=jnp.int32)
    causal = order[:, None] >= order[None, :]

    def block_step(carry, inputs):
        carried, previous = carry
        drive_block, in_block, out_block, log_block, seg_block = inputs
        cumulative = jnp.cumsum(log_block, axis=0)
        gram = jnp.dot(out_block, in_block.T, precision=HIGH)
        same = (seg_block[:, None] == seg_block[None, :]) & causal
        result = jnp.zeros((SCAN_BLOCK, channels), jnp.float32)
        for slot_index in range(2):
            column = cumulative[:, slot_index]
            spread = jnp.minimum(column[:, None] - column[None, :], 0.0)
            weights = jnp.where(same, jnp.exp(spread), 0.0)
            result = result + jnp.dot(
                gram * weights, drive_block * slot_masks[slot_index], precision=HIGH
            )
        carried_in = carried * (seg_block[0] == previous).astype(jnp.float32)
        rising = jnp.exp(cumulative[:, 0:1]) * mask_low + jnp.exp(cumulative[:, 1:2]) * mask_high
        leading = (seg_block == seg_block[0]).astype(jnp.float32)[:, None]
        result = result + leading * rising * jnp.dot(out_block, carried_in.T, precision=HIGH)
        trailing = (seg_block == seg_block[-1]).astype(jnp.float32)[:, None]
        tail_low = jnp.exp(cumulative[-1:, 0:1] - cumulative[:, 0:1])
        tail_high = jnp.exp(cumulative[-1:, 1:2] - cumulative[:, 1:2])
        tail = tail_low * mask_low + tail_high * mask_high
        whole_block = (seg_block[-1] == seg_block[0]).astype(jnp.float32)
        carried_new = whole_block * rising[-1][:, None] * carried_in + jnp.dot(
            (drive_block * tail * trailing).T, in_block, precision=HIGH
        )
        return ((carried_new, seg_block[-1]), result)

    initial = (jnp.zeros((channels, NSTATE), jnp.float32), jnp.int32(-1))
    scan_inputs = (
        driven.reshape(blocks, SCAN_BLOCK, channels),
        input_map.reshape(blocks, SCAN_BLOCK, NSTATE),
        output_map.reshape(blocks, SCAN_BLOCK, NSTATE),
        log_pair.reshape(blocks, SCAN_BLOCK, 2),
        segment.reshape(blocks, SCAN_BLOCK),
    )
    final_carry, scanned = lax.scan(block_step, initial, scan_inputs)
    mixed = scanned.reshape(tokens_all, channels) + jnp.take(d_skip, channel_head) * conv_value
    gated = mixed * jax.nn.silu(gate_half)
    squares = jnp.sum(gated * gated, axis=1)
    gained = (gated * norm_gain).astype(jnp.bfloat16)
    square_high = squares.astype(jnp.bfloat16)
    square_low = (squares - square_high.astype(jnp.float32)).astype(jnp.bfloat16)
    sent = jnp.concatenate([gained, square_high[:, None], square_low[:, None]], axis=1)
    bz = lax.axis_size("bz")
    by = lax.axis_size("by")
    bc = lax.axis_size("bc")
    sent = sent.reshape(bz, by, bc, rows_count, channels + 2)
    both = lax.all_gather(sent, "bc", axis=0)
    mine = lax.dynamic_index_in_dim(both, lax.axis_index("bc"), axis=3, keepdims=False)
    mine = jnp.transpose(mine, (2, 1, 3, 0, 4))
    half_rows = bz * by * rows_count
    gained_pair = mine[..., :channels].reshape(half_rows, bc * channels)
    squares_pair = jnp.sum(mine[..., channels:].astype(jnp.float32), axis=(3, 4)).reshape(half_rows)
    w_pair = lax.all_gather(w_out, "bc", axis=0, tiled=True)
    partial = jnp.dot(gained_pair, w_pair, preferred_element_type=jnp.float32)
    packed = jnp.concatenate(
        [partial, squares_pair[:, None], jnp.zeros((half_rows, 127), jnp.float32)], axis=1
    )
    packed = packed.reshape(by, bz, rows_count, D + 128)
    packed = lax.psum_scatter(packed, "by", scatter_dimension=0)
    packed_own = lax.psum_scatter(packed, "bz", scatter_dimension=0)
    inverse = lax.rsqrt(packed_own[:, D] / inner_total + EPSILON)
    delta_own = packed_own[:, :D] * inverse[:, None]
    layer_own = (rows_own.astype(jnp.float32) + delta_own).astype(jnp.bfloat16)
    logits = jnp.dot(
        gather_rows(final_norm(layer_own, final_gain)),
        w_head,
        preferred_element_type=jnp.float32,
    )
    vocab_local = w_head.shape[1]
    local_label = labels[0] - blk_index * vocab_local
    hit = jnp.arange(vocab_local, dtype=jnp.int32)[None, :] == local_label[:, None]
    target_local = jnp.sum(jnp.where(hit, logits, 0.0), axis=1)
    top_local = jnp.max(logits, axis=1)
    expsum_local = jnp.sum(jnp.exp(logits - top_local[:, None]), axis=1)
    top_all, expsum_all, target_all = combine_blk(top_local, expsum_local, target_local)
    logprob = target_all - (top_all + jnp.log(expsum_all))
    token_own = lax.dynamic_slice_in_dim(logprob, blk_index * rows_count, rows_count, 0)
    seqs_count = lengths.shape[1]
    onehot = (segment[:, None] == jnp.arange(seqs_count, dtype=jnp.int32)[None, :]).astype(
        jnp.float32
    )
    sums = jnp.dot(logprob, onehot, precision=HIGH)
    seq_index = lax.axis_index("seq")
    mine = lax.dynamic_slice_in_dim(owners, seq_index * seqs_count, seqs_count, 0)
    placement = (mine[:, None] == jnp.arange(owners.shape[0], dtype=jnp.int32)[None, :]).astype(
        jnp.float32
    )
    spread_sums = jnp.dot(sums, placement, precision=HIGH)
    seq_own = lax.psum_scatter(spread_sums, "seq", scatter_dimension=0, tiled=True)
    return (layer_own[None], token_own[None], seq_own)


def solution(mesh):
    blk = mesh.shape["blk"]
    split = mesh.devices.reshape((blk // 16, 8, 2) + mesh.devices.shape[1:])
    mesh = Mesh(split, BLK + mesh.axis_names[1:])
    in_specs = (
        P(("mp", "seq"), BLK, None),
        P("seq", None),
        P("seq", None),
        P(),
        P("mp", None, BLK),
        P("mp", None),
        P("mp", BLK),
        P("mp", None),
        P("mp"),
        P("mp"),
        P("mp"),
        P(("mp",) + BLK),
        P(("mp",) + BLK, None),
        P("mp"),
        P("mp", BLK),
    )
    out_specs = (P(("mp", "seq"), BLK, None), P(("mp", "seq"), BLK), P(("mp", "seq")))
    return jax.shard_map(shards, mesh=mesh, in_specs=in_specs, out_specs=out_specs, check_vma=False)
```

```python
import jax
import jax.numpy as jnp
from jax import lax
from jax.sharding import Mesh
from jax.sharding import PartitionSpec as P

D = 1536
HEADDIM = 64
NSTATE = 128
SCAN_BLOCK = 512
CONV = 4


EPSILON = 1e-05
HIGH = lax.Precision.HIGHEST
BLK = ("bz", "by", "bc")


def gather_rows(rows):
    count = lax.axis_size("bz")
    here = lax.axis_index("bz")
    moved = [rows] + [
        lax.ppermute(rows, "bz", [(i, (i + shift) % count) for i in range(count)])
        for shift in range(1, count)
    ]
    part = jnp.take(jnp.stack(moved), (here - jnp.arange(count)) % count, axis=0)
    part = lax.all_gather(part, ("by", "bc"), axis=1)
    return part.reshape((-1,) + rows.shape[1:])


def scatter_rows(values):
    bz = lax.axis_size("bz")
    by = lax.axis_size("by")
    bc = lax.axis_size("bc")
    part = values.reshape((bz, by, bc, -1) + values.shape[1:])
    part = lax.psum_scatter(part, "bc", scatter_dimension=2)
    part = lax.psum_scatter(part, "by", scatter_dimension=1)
    return lax.psum_scatter(part, "bz", scatter_dimension=0)


def sum_blk(values):
    return lax.psum(lax.psum(lax.psum(values, "bc"), "by"), "bz")


def combine_blk(top, expsum, target):
    for axis in (("by", "bc"), "bz"):
        pieces = lax.all_gather(jnp.stack([top, expsum, target]), axis, axis=0)
        top = jnp.max(pieces[:, 0], axis=0)
        expsum = jnp.sum(pieces[:, 1] * jnp.exp(pieces[:, 0] - top[None]), axis=0)
        target = jnp.sum(pieces[:, 2], axis=0)
    return top, expsum, target


def segments_of(lengths, count):
    starts = jnp.cumsum(lengths, axis=-1) - lengths
    places = jnp.arange(count, dtype=jnp.int32)
    segment = jnp.sum((places[:, None] >= starts[None, :]).astype(jnp.int32), axis=-1) - 1
    first = jnp.take(starts, segment)
    return (segment, places - first)


def causal_conv(values, weights, position):
    total = values * weights[0]
    for shift_by in range(1, CONV):
        moved = jnp.concatenate(
            [jnp.zeros_like(values[:shift_by, :]), values[:-shift_by, :]], axis=0
        )
        total = (
            total + moved * weights[shift_by] * (position >= shift_by).astype(jnp.float32)[:, None]
        )
    return total


def final_norm(values, gain):
    widened = values.astype(jnp.float32)
    scale = lax.rsqrt(jnp.mean(widened * widened, axis=-1, keepdims=True) + EPSILON)
    return (widened * scale * gain).astype(jnp.bfloat16)


def shards(
    hidden,
    labels,
    lengths,
    owners,
    w_inner,
    w_bcdt,
    conv_inner,
    conv_bc,
    dt_bias,
    decay_rate,
    d_skip,
    norm_gain,
    w_out,
    final_gain,
    w_head,
):
    rows_own = hidden[0]
    rows_count = rows_own.shape[0]
    blk_count = lax.axis_size("bz") * lax.axis_size("by") * lax.axis_size("bc")
    blk_index = (
        lax.axis_index("bz") * lax.axis_size("by") + lax.axis_index("by")
    ) * lax.axis_size("bc") + lax.axis_index("bc")
    gathered = gather_rows(rows_own)
    tokens_all = gathered.shape[0]
    channels = w_inner.shape[2]
    inner_total = channels * blk_count
    inner_proj = jnp.dot(
        gathered, w_inner.reshape(D, 2 * channels), preferred_element_type=jnp.float32
    ).astype(jnp.bfloat16)
    state_proj = jnp.dot(gathered, w_bcdt, preferred_element_type=jnp.float32).astype(jnp.bfloat16)
    gate_half = inner_proj[:, :channels].astype(jnp.float32)
    segment, position = segments_of(lengths[0], tokens_all)
    conv_value = jax.nn.silu(
        causal_conv(inner_proj[:, channels:].astype(jnp.float32), conv_inner, position)
    )
    conv_state = jax.nn.silu(
        causal_conv(state_proj[:, : 2 * NSTATE].astype(jnp.float32), conv_bc, position)
    )
    input_map = conv_state[:, :NSTATE]
    output_map = conv_state[:, NSTATE:]
    step_size = jax.nn.softplus(state_proj[:, 2 * NSTATE :].astype(jnp.float32) + dt_bias)
    log_heads = -(step_size * decay_rate)
    first_channel = blk_index * channels
    channel_head = (first_channel + jnp.arange(channels, dtype=jnp.int32)) // HEADDIM
    head_low = first_channel // HEADDIM
    head_high = (first_channel + channels - 1) // HEADDIM
    mask_high = (channel_head == head_high).astype(jnp.float32)
    mask_low = 1.0 - mask_high
    step_pair = jnp.concatenate(
        [
            lax.dynamic_slice_in_dim(step_size, head_low, 1, 1),
            lax.dynamic_slice_in_dim(step_size, head_high, 1, 1),
        ],
        axis=1,
    )
    log_pair = jnp.concatenate(
        [
            lax.dynamic_slice_in_dim(log_heads, head_low, 1, 1),
            lax.dynamic_slice_in_dim(log_heads, head_high, 1, 1),
        ],
        axis=1,
    )
    step_channel = step_pair[:, 0:1] * mask_low + step_pair[:, 1:2] * mask_high
    driven = conv_value * step_channel
    slot_masks = (mask_low, mask_high)
    blocks = tokens_all // SCAN_BLOCK
    order = jnp.arange(SCAN_BLOCK, dtype=jnp.int32)
    causal = order[:, None] >= order[None, :]

    def block_step(carry, inputs):
        carried, previous = carry
        drive_block, in_block, out_block, log_block, seg_block = inputs
        cumulative = jnp.cumsum(log_block, axis=0)
        gram = jnp.dot(out_block, in_block.T, precision=HIGH)
        same = (seg_block[:, None] == seg_block[None, :]) & causal
        result = jnp.zeros((SCAN_BLOCK, channels), jnp.float32)
        for slot_index in range(2):
            column = cumulative[:, slot_index]
            spread = jnp.minimum(column[:, None] - column[None, :], 0.0)
            weights = jnp.where(same, jnp.exp(spread), 0.0)
            result = result + jnp.dot(
                gram * weights, drive_block * slot_masks[slot_index], precision=HIGH
            )
        carried_in = carried * (seg_block[0] == previous).astype(jnp.float32)
        rising = jnp.exp(cumulative[:, 0:1]) * mask_low + jnp.exp(cumulative[:, 1:2]) * mask_high
        leading = (seg_block == seg_block[0]).astype(jnp.float32)[:, None]
        result = result + leading * rising * jnp.dot(out_block, carried_in.T, precision=HIGH)
        trailing = (seg_block == seg_block[-1]).astype(jnp.float32)[:, None]
        tail_low = jnp.exp(cumulative[-1:, 0:1] - cumulative[:, 0:1])
        tail_high = jnp.exp(cumulative[-1:, 1:2] - cumulative[:, 1:2])
        tail = tail_low * mask_low + tail_high * mask_high
        whole_block = (seg_block[-1] == seg_block[0]).astype(jnp.float32)
        carried_new = whole_block * rising[-1][:, None] * carried_in + jnp.dot(
            (drive_block * tail * trailing).T, in_block, precision=HIGH
        )
        return ((carried_new, seg_block[-1]), result)

    initial = (jnp.zeros((channels, NSTATE), jnp.float32), jnp.int32(-1))
    scan_inputs = (
        driven.reshape(blocks, SCAN_BLOCK, channels),
        input_map.reshape(blocks, SCAN_BLOCK, NSTATE),
        output_map.reshape(blocks, SCAN_BLOCK, NSTATE),
        log_pair.reshape(blocks, SCAN_BLOCK, 2),
        segment.reshape(blocks, SCAN_BLOCK),
    )
    final_carry, scanned = lax.scan(block_step, initial, scan_inputs)
    mixed = scanned.reshape(tokens_all, channels) + jnp.take(d_skip, channel_head) * conv_value
    gated = mixed * jax.nn.silu(gate_half)
    squares = jnp.sum(gated * gated, axis=1)
    gained = (gated * norm_gain).astype(jnp.bfloat16)
    square_high = squares.astype(jnp.bfloat16)
    square_low = (squares - square_high.astype(jnp.float32)).astype(jnp.bfloat16)
    sent = jnp.concatenate([gained, square_high[:, None], square_low[:, None]], axis=1)
    bz = lax.axis_size("bz")
    by = lax.axis_size("by")
    bc = lax.axis_size("bc")
    sent = sent.reshape(bz, by, bc, rows_count, channels + 2)
    both = lax.all_gather(sent, "bc", axis=0)
    mine = lax.dynamic_index_in_dim(both, lax.axis_index("bc"), axis=3, keepdims=False)
    mine = jnp.transpose(mine, (2, 1, 3, 0, 4))
    half_rows = bz * by * rows_count
    gained_pair = mine[..., :channels].reshape(half_rows, bc * channels)
    squares_pair = jnp.sum(mine[..., channels:].astype(jnp.float32), axis=(3, 4)).reshape(half_rows)
    w_pair = lax.all_gather(w_out, "bc", axis=0, tiled=True)
    partial = jnp.dot(gained_pair, w_pair, preferred_element_type=jnp.float32)
    packed = jnp.concatenate(
        [partial, squares_pair[:, None], jnp.zeros((half_rows, 127), jnp.float32)], axis=1
    )
    packed = packed.reshape(by, bz, rows_count, D + 128)
    packed = lax.psum_scatter(packed, "by", scatter_dimension=0)
    packed_own = lax.psum_scatter(packed, "bz", scatter_dimension=0)
    inverse = lax.rsqrt(packed_own[:, D] / inner_total + EPSILON)
    delta_own = packed_own[:, :D] * inverse[:, None]
    layer_own = (rows_own.astype(jnp.float32) + delta_own).astype(jnp.bfloat16)
    logits = jnp.dot(
        gather_rows(final_norm(layer_own, final_gain)),
        w_head,
        preferred_element_type=jnp.float32,
    )
    vocab_local = w_head.shape[1]
    local_label = labels[0] - blk_index * vocab_local
    hit = jnp.arange(vocab_local, dtype=jnp.int32)[None, :] == local_label[:, None]
    target_local = jnp.sum(jnp.where(hit, logits, 0.0), axis=1)
    top_local = jnp.max(logits, axis=1)
    expsum_local = jnp.sum(jnp.exp(logits - top_local[:, None]), axis=1)
    top_all, expsum_all, target_all = combine_blk(top_local, expsum_local, target_local)
    logprob = target_all - (top_all + jnp.log(expsum_all))
    token_own = lax.dynamic_slice_in_dim(logprob, blk_index * rows_count, rows_count, 0)
    seqs_count = lengths.shape[1]
    onehot = (segment[:, None] == jnp.arange(seqs_count, dtype=jnp.int32)[None, :]).astype(
        jnp.float32
    )
    sums = jnp.dot(logprob, onehot, precision=HIGH)
    seq_index = lax.axis_index("seq")
    mine = lax.dynamic_slice_in_dim(owners, seq_index * seqs_count, seqs_count, 0)
    placement = (mine[:, None] == jnp.arange(owners.shape[0], dtype=jnp.int32)[None, :]).astype(
        jnp.float32
    )
    spread_sums = jnp.dot(sums, placement, precision=HIGH)
    seq_own = lax.psum_scatter(spread_sums, "seq", scatter_dimension=0, tiled=True)
    return (layer_own[None], token_own[None], seq_own)


def solution(mesh):
    blk = mesh.shape["blk"]
    split = mesh.devices.reshape((blk // 16, 8, 2) + mesh.devices.shape[1:])
    mesh = Mesh(split, BLK + mesh.axis_names[1:])
    in_specs = (
        P(("mp", "seq"), BLK, None),
        P("seq", None),
        P("seq", None),
        P(),
        P("mp", None, BLK),
        P("mp", None),
        P("mp", BLK),
        P("mp", None),
        P("mp"),
        P("mp"),
        P("mp"),
        P(("mp",) + BLK),
        P(("mp",) + BLK, None),
        P("mp"),
        P("mp", BLK),
    )
    out_specs = (P(("mp", "seq"), BLK, None), P(("mp", "seq"), BLK), P(("mp", "seq")))
    return jax.shard_map(shards, mesh=mesh, in_specs=in_specs, out_specs=out_specs, check_vma=False)
```

```python
import jax
import jax.numpy as jnp
from jax import lax
from jax.sharding import Mesh
from jax.sharding import PartitionSpec as P

D = 1536
HEADDIM = 64
NSTATE = 128
SCAN_BLOCK = 512
CONV = 4


EPSILON = 1e-05
HIGH = lax.Precision.HIGHEST
BLK = ("bz", "by", "bc")


def gather_rows(rows):
    part = lax.all_gather(rows, "bz", axis=0)
    part = lax.all_gather(part, ("by", "bc"), axis=1)
    return part.reshape((-1,) + rows.shape[1:])


def scatter_rows(values):
    bz = lax.axis_size("bz")
    by = lax.axis_size("by")
    bc = lax.axis_size("bc")
    part = values.reshape((bz, by, bc, -1) + values.shape[1:])
    part = lax.psum_scatter(part, "bc", scatter_dimension=2)
    part = lax.psum_scatter(part, "by", scatter_dimension=1)
    return lax.psum_scatter(part, "bz", scatter_dimension=0)


def sum_blk(values):
    return lax.psum(lax.psum(lax.psum(values, "bc"), "by"), "bz")


def merge_pieces(pieces):
    top = jnp.max(pieces[:, 0], axis=0)
    expsum = jnp.sum(pieces[:, 1] * jnp.exp(pieces[:, 0] - top[None]), axis=0)
    return top, expsum, jnp.sum(pieces[:, 2], axis=0)


def combine_blk(top, expsum, target):
    for axis in (("by", "bc"), "bz"):
        pieces = lax.all_gather(jnp.stack([top, expsum, target]), axis, axis=0)
        top = jnp.max(pieces[:, 0], axis=0)
        expsum = jnp.sum(pieces[:, 1] * jnp.exp(pieces[:, 0] - top[None]), axis=0)
        target = jnp.sum(pieces[:, 2], axis=0)
    return top, expsum, target


def segments_of(lengths, count):
    starts = jnp.cumsum(lengths, axis=-1) - lengths
    places = jnp.arange(count, dtype=jnp.int32)
    segment = jnp.sum((places[:, None] >= starts[None, :]).astype(jnp.int32), axis=-1) - 1
    first = jnp.take(starts, segment)
    return (segment, places - first)


def causal_conv(values, weights, position):
    total = values * weights[0]
    for shift_by in range(1, CONV):
        moved = jnp.concatenate(
            [jnp.zeros_like(values[:shift_by, :]), values[:-shift_by, :]], axis=0
        )
        total = (
            total + moved * weights[shift_by] * (position >= shift_by).astype(jnp.float32)[:, None]
        )
    return total


def final_norm(values, gain):
    widened = values.astype(jnp.float32)
    scale = lax.rsqrt(jnp.mean(widened * widened, axis=-1, keepdims=True) + EPSILON)
    return (widened * scale * gain).astype(jnp.bfloat16)


def shards(
    hidden,
    labels,
    lengths,
    owners,
    w_inner,
    w_bcdt,
    conv_inner,
    conv_bc,
    dt_bias,
    decay_rate,
    d_skip,
    norm_gain,
    w_out,
    final_gain,
    w_head,
):
    rows_own = hidden[0]
    rows_count = rows_own.shape[0]
    blk_count = lax.axis_size("bz") * lax.axis_size("by") * lax.axis_size("bc")
    blk_index = (
        lax.axis_index("bz") * lax.axis_size("by") + lax.axis_index("by")
    ) * lax.axis_size("bc") + lax.axis_index("bc")
    gathered = gather_rows(rows_own)
    tokens_all = gathered.shape[0]
    channels = w_inner.shape[2]
    inner_total = channels * blk_count
    inner_proj = jnp.dot(
        gathered, w_inner.reshape(D, 2 * channels), preferred_element_type=jnp.float32
    ).astype(jnp.bfloat16)
    state_proj = jnp.dot(gathered, w_bcdt, preferred_element_type=jnp.float32).astype(jnp.bfloat16)
    gate_half = inner_proj[:, :channels].astype(jnp.float32)
    segment, position = segments_of(lengths[0], tokens_all)
    conv_value = jax.nn.silu(
        causal_conv(inner_proj[:, channels:].astype(jnp.float32), conv_inner, position)
    )
    conv_state = jax.nn.silu(
        causal_conv(state_proj[:, : 2 * NSTATE].astype(jnp.float32), conv_bc, position)
    )
    input_map = conv_state[:, :NSTATE]
    output_map = conv_state[:, NSTATE:]
    step_size = jax.nn.softplus(state_proj[:, 2 * NSTATE :].astype(jnp.float32) + dt_bias)
    log_heads = -(step_size * decay_rate)
    first_channel = blk_index * channels
    channel_head = (first_channel + jnp.arange(channels, dtype=jnp.int32)) // HEADDIM
    head_low = first_channel // HEADDIM
    head_high = (first_channel + channels - 1) // HEADDIM
    mask_high = (channel_head == head_high).astype(jnp.float32)
    mask_low = 1.0 - mask_high
    step_pair = jnp.concatenate(
        [
            lax.dynamic_slice_in_dim(step_size, head_low, 1, 1),
            lax.dynamic_slice_in_dim(step_size, head_high, 1, 1),
        ],
        axis=1,
    )
    log_pair = jnp.concatenate(
        [
            lax.dynamic_slice_in_dim(log_heads, head_low, 1, 1),
            lax.dynamic_slice_in_dim(log_heads, head_high, 1, 1),
        ],
        axis=1,
    )
    step_channel = step_pair[:, 0:1] * mask_low + step_pair[:, 1:2] * mask_high
    driven = conv_value * step_channel
    slot_masks = (mask_low, mask_high)
    blocks = tokens_all // SCAN_BLOCK
    order = jnp.arange(SCAN_BLOCK, dtype=jnp.int32)
    causal = order[:, None] >= order[None, :]

    def block_step(carry, inputs):
        carried, previous = carry
        drive_block, in_block, out_block, log_block, seg_block = inputs
        cumulative = jnp.cumsum(log_block, axis=0)
        gram = jnp.dot(out_block, in_block.T, precision=HIGH)
        same = (seg_block[:, None] == seg_block[None, :]) & causal
        result = jnp.zeros((SCAN_BLOCK, channels), jnp.float32)
        for slot_index in range(2):
            column = cumulative[:, slot_index]
            spread = jnp.minimum(column[:, None] - column[None, :], 0.0)
            weights = jnp.where(same, jnp.exp(spread), 0.0)
            result = result + jnp.dot(
                gram * weights, drive_block * slot_masks[slot_index], precision=HIGH
            )
        carried_in = carried * (seg_block[0] == previous).astype(jnp.float32)
        rising = jnp.exp(cumulative[:, 0:1]) * mask_low + jnp.exp(cumulative[:, 1:2]) * mask_high
        leading = (seg_block == seg_block[0]).astype(jnp.float32)[:, None]
        result = result + leading * rising * jnp.dot(out_block, carried_in.T, precision=HIGH)
        trailing = (seg_block == seg_block[-1]).astype(jnp.float32)[:, None]
        tail_low = jnp.exp(cumulative[-1:, 0:1] - cumulative[:, 0:1])
        tail_high = jnp.exp(cumulative[-1:, 1:2] - cumulative[:, 1:2])
        tail = tail_low * mask_low + tail_high * mask_high
        whole_block = (seg_block[-1] == seg_block[0]).astype(jnp.float32)
        carried_new = whole_block * rising[-1][:, None] * carried_in + jnp.dot(
            (drive_block * tail * trailing).T, in_block, precision=HIGH
        )
        return ((carried_new, seg_block[-1]), result)

    initial = (jnp.zeros((channels, NSTATE), jnp.float32), jnp.int32(-1))
    scan_inputs = (
        driven.reshape(blocks, SCAN_BLOCK, channels),
        input_map.reshape(blocks, SCAN_BLOCK, NSTATE),
        output_map.reshape(blocks, SCAN_BLOCK, NSTATE),
        log_pair.reshape(blocks, SCAN_BLOCK, 2),
        segment.reshape(blocks, SCAN_BLOCK),
    )
    final_carry, scanned = lax.scan(block_step, initial, scan_inputs)
    mixed = scanned.reshape(tokens_all, channels) + jnp.take(d_skip, channel_head) * conv_value
    gated = mixed * jax.nn.silu(gate_half)
    squares = jnp.sum(gated * gated, axis=1)
    gained = (gated * norm_gain).astype(jnp.bfloat16)
    square_high = squares.astype(jnp.bfloat16)
    square_low = (squares - square_high.astype(jnp.float32)).astype(jnp.bfloat16)
    sent = jnp.concatenate([gained, square_high[:, None], square_low[:, None]], axis=1)
    bz = lax.axis_size("bz")
    by = lax.axis_size("by")
    bc = lax.axis_size("bc")
    sent = sent.reshape(bz, by, bc, rows_count, channels + 2)
    both = lax.all_gather(sent, "bc", axis=0)
    mine = lax.dynamic_index_in_dim(both, lax.axis_index("bc"), axis=3, keepdims=False)
    mine = jnp.transpose(mine, (2, 1, 3, 0, 4))
    half_rows = bz * by * rows_count
    gained_pair = mine[..., :channels].reshape(half_rows, bc * channels)
    squares_pair = jnp.sum(mine[..., channels:].astype(jnp.float32), axis=(3, 4)).reshape(half_rows)
    w_pair = lax.all_gather(w_out, "bc", axis=0, tiled=True)
    partial = jnp.dot(gained_pair, w_pair, preferred_element_type=jnp.float32)
    packed = jnp.concatenate(
        [partial, squares_pair[:, None], jnp.zeros((half_rows, 127), jnp.float32)], axis=1
    )
    packed = packed.reshape(by, bz, rows_count, D + 128)
    packed = lax.psum_scatter(packed, "by", scatter_dimension=0)
    packed_own = lax.psum_scatter(packed, "bz", scatter_dimension=0)
    inverse = lax.rsqrt(packed_own[:, D] / inner_total + EPSILON)
    delta_own = packed_own[:, :D] * inverse[:, None]
    layer_own = (rows_own.astype(jnp.float32) + delta_own).astype(jnp.bfloat16)
    logits = jnp.dot(
        gather_rows(final_norm(layer_own, final_gain)),
        w_head,
        preferred_element_type=jnp.float32,
    )
    vocab_local = w_head.shape[1]
    local_label = labels[0] - blk_index * vocab_local
    hit = jnp.arange(vocab_local, dtype=jnp.int32)[None, :] == local_label[:, None]
    target_local = jnp.sum(jnp.where(hit, logits, 0.0), axis=1)
    top_local = jnp.max(logits, axis=1)
    expsum_local = jnp.sum(jnp.exp(logits - top_local[:, None]), axis=1)
    top, expsum, target = merge_pieces(
        lax.all_gather(jnp.stack([top_local, expsum_local, target_local]), ("by", "bc"), axis=0)
    )
    seqs_count = lengths.shape[1]
    groups = lax.axis_size("seq")
    seq_index = lax.axis_index("seq")
    payload = jnp.stack([top, expsum, target, segment.astype(jnp.float32)])
    every = lax.all_gather(payload, ("bz", "seq"), axis=0)
    every = every.reshape(lax.axis_size("bz"), groups, 4, tokens_all)
    top_g, expsum_g, target_g = merge_pieces(jnp.moveaxis(every[:, :, :3], 2, 1))
    segment_g = every[0, :, 3]
    logprob_g = target_g - (top_g + jnp.log(expsum_g))
    logprob = lax.dynamic_index_in_dim(logprob_g, seq_index, axis=0, keepdims=False)
    token_own = lax.dynamic_slice_in_dim(logprob, blk_index * rows_count, rows_count, 0)
    onehot = (
        segment_g[:, :, None] == jnp.arange(seqs_count, dtype=jnp.float32)[None, None, :]
    ).astype(jnp.float32)
    sums = jnp.einsum("gt,gtk->gk", logprob_g, onehot, precision=HIGH).reshape(-1)
    slots = seq_index * seqs_count + jnp.arange(seqs_count, dtype=jnp.int32)
    placement = (owners[:, None] == slots[None, :]).astype(jnp.float32)
    seq_own = jnp.dot(sums, placement, precision=HIGH)
    return (layer_own[None], token_own[None], seq_own)


def solution(mesh):
    blk = mesh.shape["blk"]
    split = mesh.devices.reshape((blk // 16, 8, 2) + mesh.devices.shape[1:])
    mesh = Mesh(split, BLK + mesh.axis_names[1:])
    in_specs = (
        P(("mp", "seq"), BLK, None),
        P("seq", None),
        P("seq", None),
        P(),
        P("mp", None, BLK),
        P("mp", None),
        P("mp", BLK),
        P("mp", None),
        P("mp"),
        P("mp"),
        P("mp"),
        P(("mp",) + BLK),
        P(("mp",) + BLK, None),
        P("mp"),
        P("mp", BLK),
    )
    out_specs = (P(("mp", "seq"), BLK, None), P(("mp", "seq"), BLK), P(("mp", "seq")))
    return jax.shard_map(shards, mesh=mesh, in_specs=in_specs, out_specs=out_specs, check_vma=False)
```
